32 devices in a mesh: dp: 8 (over z, x), vocab: 4 (over y, core).
Axes of the slice: x: 2, y: 2, z: 4, core: 2. Of those that a mesh axis runs over, the one named last changes fastest.
Arguments:
- hidden: bfloat16 [4096, 4096], P(('dp', 'vocab')), may hold values from -6 to 6
- positions: int32 [32, 6], P(('dp', 'vocab')), may hold values from 0 to 127, as said below
- counts: int32 [32], P(('dp', 'vocab')), may hold values from 0 to 6, as said below
- targets: int32 [32, 6], P(('dp', 'vocab')), may hold values from 0 to 131071
- dense_weight: bfloat16 [4096, 4096], P('dp', 'vocab'), may hold values from -0.09375 to 0.09375
- dense_bias: float32 [4096], P('vocab'), may hold values from -3 to 3
- norm_gain: float32 [4096], P('vocab'), may hold values from 0.5 to 1.5
- norm_shift: float32 [4096], P('vocab'), may hold values from -3 to 3
- embedding: bfloat16 [131072, 4096], P(('dp', 'vocab')), as said below
- decoder_bias: float32 [131072], P(('dp', 'vocab')), may hold values from -6 to 6
Outputs:
- emb_grad: bfloat16 [131072, 4096], P(('dp', 'vocab'))
- bias_grad: float32 [131072], P(('dp', 'vocab'))
- row_loss: float32 [64], replicated
The draws below stay inside these ranges and needn't reach their ends.
Inputs may be any that keep to these rules, and one draw needn't show every extreme that they name: Each micro-batch's counts sum to exactly 8; in every micro-batch one device has exactly 6. `positions`: A device's list holds distinct rows of its own block. `embedding`: entries lie within 302 / sqrt(4096) in magnitude.
All inputs are finite; a program needn't handle non-finite values.
Results may differ from the reference program's by a relative error of at most 0.0085.
Values may be sent and summed in bfloat16 or wider, within the bound.
No kernel may reach another device: no remote copies, remote signals or barrier semaphores. Data moves between devices by JAX's collectives and lax.ppermute only.
A program may use at most 128 MiB of HBM per device.

```python
import math
import jax
import jax.numpy as jnp
from jax import lax

D = 4096
VOCAB = 131072
TOK_DEV = 128
MEAN = 2
MAXM = 6
GROUPM = 8
TOKENS = 4096
N_DP = 8
N_VOCAB = 4


def draw_counts(key, part):
    keys = jax.random.split(jax.random.fold_in(key, 7), N_DP)

    def one_group(group_key):
        first_key, second_key = jax.random.split(group_key)
        fullest = jax.random.randint(first_key, (), 0, N_VOCAB)
        units = MEAN * (N_VOCAB - 3)
        order = jax.random.permutation(second_key, (N_VOCAB - 1) * MAXM)
        owner = order[:units] // MAXM
        others = jnp.sum((owner[:, None] == jnp.arange(N_VOCAB - 1)[None, :]).astype(jnp.int32), axis=0)
        device = jnp.arange(N_VOCAB)
        which = jnp.clip(device - (device > fullest).astype(jnp.int32), 0, N_VOCAB - 2)
        return jnp.where(device == fullest, MAXM, others[which]).astype(jnp.int32)
    return jax.vmap(one_group)(keys).reshape(-1).astype(jnp.int32)


def draw_positions(key, part):
    keys = jax.random.split(jax.random.fold_in(key, 11), N_DP * N_VOCAB)

    def one_device(device_key):
        return jax.random.permutation(device_key, TOK_DEV)[:MAXM].astype(jnp.int32)
    return jax.vmap(one_device)(keys)


def draw_embedding(key, part):
    first_key, second_key = jax.random.split(jax.random.fold_in(key, 13))
    normal_part = jnp.clip(jax.random.normal(first_key, (VOCAB, D), jnp.float32), -5.0, 5.0)
    row_scale = jnp.exp(jax.random.uniform(second_key, (VOCAB, 1), jnp.float32, 0.0, math.log(6.0)))
    weights = normal_part * row_scale * (1.0 / math.sqrt(D))
    return weights.astype(jnp.bfloat16)


def with_ends(drawn, stream_key, smallest, top_value):
    spot = [jax.random.randint(jax.random.fold_in(stream_key, axis), (), 0, length) for axis, length in enumerate(drawn.shape)]
    widest = drawn.shape.index(max(drawn.shape))
    neighbour = spot[:widest] + [(spot[widest] + 1) % drawn.shape[widest]] + spot[widest + 1:]
    return drawn.at[tuple(spot)].set(smallest).at[tuple(neighbour)].set(top_value)


def levels(key, dims, cuts, least, high):
    def one(axis_at, shards_of):
        draws = jax.random.uniform(jax.random.fold_in(jax.random.fold_in(key, 6), axis_at), (shards_of,), jnp.float32, least / len(cuts), high / len(cuts))
        return jnp.repeat(jnp.exp(draws), dims[axis_at] // shards_of).reshape((-1,) + (1,) * (len(dims) - axis_at - 1))

    factor_of = one(*cuts[0])
    for cut in cuts[1:]:
        factor_of = factor_of * one(*cut)
    return factor_of


def gaussian(key, extent, scale, limit, shards=(), held_as=jnp.bfloat16):
    loudness = levels(key, extent, shards, -0.22, 0.18) if shards else 1.0
    entries = jax.random.normal(key, extent, jnp.float32) * scale * loudness
    return jnp.minimum(jnp.maximum(entries, -limit), limit).astype(held_as)


def setup_inputs(seed: int = 0) -> dict:
    splits = jax.random.split(jax.random.key(seed), 11)
    hidden = gaussian(splits[0], (TOKENS, D), 1.0, 6.0, ((0, 32),))
    positions = draw_positions(jax.random.fold_in(splits[10], 71), 0)
    counts = draw_counts(jax.random.fold_in(splits[10], 71), 0)
    targets = with_ends(jax.random.randint(splits[3], (N_DP * N_VOCAB, MAXM), 0, VOCAB), jax.random.fold_in(splits[3], 1), 0, VOCAB - 1).astype(jnp.int32)
    dense_weight = gaussian(splits[4], (D, D), D ** -0.5, 0.09375, ((0, 8), (1, 4)))
    dense_bias = gaussian(splits[5], (D,), 0.5, 3.0, ((0, 4),), jnp.float32)
    norm_gain = jnp.clip(1.0 + 0.1 * jax.random.normal(splits[6], (D,), jnp.float32), 0.5, 1.5)
    norm_shift = gaussian(splits[7], (D,), 0.5, 3.0, ((0, 4),), jnp.float32)
    embedding = draw_embedding(jax.random.fold_in(splits[10], 71), 0)
    decoder_bias = gaussian(splits[9], (VOCAB,), 1.0, 6.0, ((0, 32),), jnp.float32)
    return dict(hidden=hidden, positions=positions, counts=counts, targets=targets, dense_weight=dense_weight, dense_bias=dense_bias, norm_gain=norm_gain, norm_shift=norm_shift, embedding=embedding, decoder_bias=decoder_bias)


EPS = 1e-05

def reference(hidden, positions, counts, targets, dense_weight, dense_bias, norm_gain, norm_shift, embedding, decoder_bias):
    devices = N_DP * N_VOCAB
    total_rows = N_DP * GROUPM
    blocks = hidden.reshape(devices, TOK_DEV, D)
    picked = jnp.take_along_axis(blocks, positions[:, :, None].astype(jnp.int32), axis=1)
    slot_ids = jnp.arange(MAXM, dtype=jnp.int32)
    valid = (slot_ids[None, :] < counts[:, None]).reshape(N_DP, N_VOCAB * MAXM).astype(jnp.int32)
    dest = jnp.cumsum(valid, axis=1) - 1
    base = (jnp.arange(N_DP, dtype=jnp.int32) * GROUPM)[:, None]
    where_to = jnp.where(valid > 0, dest + base, total_rows).reshape(-1).astype(jnp.int32)
    rows = jnp.zeros((total_rows, D), jnp.bfloat16).at[where_to].set(picked.reshape(-1, D), mode='drop')
    tgt = jnp.zeros((total_rows,), jnp.int32).at[where_to].set(targets.reshape(-1), mode='drop')
    act = jnp.dot(rows, dense_weight, preferred_element_type=jnp.float32) + dense_bias
    act = jax.nn.gelu(act, approximate=False)
    mean = lax.optimization_barrier(jnp.sum(act, axis=1, keepdims=True)) / D
    var = lax.optimization_barrier(jnp.sum(act * act, axis=1, keepdims=True)) / D - mean * mean
    head = ((act - mean) * lax.rsqrt(var + EPS) * norm_gain + norm_shift).astype(jnp.bfloat16)
    nblocks = 32
    width = VOCAB // nblocks
    emb_blocks = embedding.reshape(nblocks, width, D)
    bias_blocks = decoder_bias.reshape(nblocks, width)
    starts = jnp.arange(nblocks, dtype=jnp.int32) * width

    def first(carry, item):
        peak, total, target_logit = carry
        emb_block, bias_block, start = item
        logits = jnp.dot(head, emb_block.T, preferred_element_type=jnp.float32) + bias_block[None, :]
        ids = start + jnp.arange(width, dtype=jnp.int32)
        newpeak = jnp.maximum(peak, lax.optimization_barrier(jnp.max(logits, axis=1)))
        total = total * jnp.exp(peak - newpeak) + lax.optimization_barrier(jnp.sum(jnp.exp(logits - newpeak[:, None]), axis=1))
        target_logit = target_logit + lax.optimization_barrier(jnp.sum(jnp.where(tgt[:, None] == ids[None, :], logits, 0.0), axis=1))
        return ((newpeak, total, target_logit), None)
    init = (jnp.full((total_rows,), -1e+30, jnp.float32), jnp.zeros((total_rows,), jnp.float32), jnp.zeros((total_rows,), jnp.float32))
    (peak, total, target_logit), _ = lax.scan(first, init, (emb_blocks, bias_blocks, starts))
    lse = peak + jnp.log(total)
    row_loss = lse - target_logit

    def second(item):
        emb_block, bias_block, start = item
        logits = jnp.dot(head, emb_block.T, preferred_element_type=jnp.float32) + bias_block[None, :]
        ids = start + jnp.arange(width, dtype=jnp.int32)
        hit = (tgt[:, None] == ids[None, :]).astype(jnp.float32)
        diff = jnp.exp(logits - lse[:, None]) - hit
        grad = (diff / total_rows).astype(jnp.bfloat16)
        emb_part = jnp.dot(grad.T, head, preferred_element_type=jnp.float32).astype(jnp.bfloat16)
        return (emb_part, lax.optimization_barrier(jnp.sum(diff, axis=0)) / total_rows)
    emb_parts, bias_parts = lax.map(second, (emb_blocks, bias_blocks, starts))
    return (emb_parts.reshape(VOCAB, D), bias_parts.reshape(VOCAB), row_loss)
```

```python
import jax
import jax.numpy as jnp
from jax import lax
from jax.sharding import PartitionSpec as P

MEAN = 2


EPS = 1e-05


def _pow2(n):
    return n & (n - 1) == 0


def _canon(axis, step, mine, theirs):
    upper = (lax.axis_index(axis) & step) != 0
    return jnp.where(upper, theirs, mine), jnp.where(upper, mine, theirs)


def _allreduce(x, axis, n, merge):
    step = 1
    while step < n:
        theirs = lax.ppermute(x, axis, [(a, a ^ step) for a in range(n)])
        lo, hi = _canon(axis, step, x, theirs)
        x = merge(lo, hi)
        step *= 2
    return x


def _allgather(x, axis, n):
    buf = x[None]
    step = 1
    while step < n:
        theirs = lax.ppermute(buf, axis, [(a, a ^ step) for a in range(n)])
        upper = (lax.axis_index(axis) & step) != 0
        buf = jnp.where(upper, jnp.concatenate([theirs, buf]), jnp.concatenate([buf, theirs]))
        step *= 2
    return buf


def _add(lo, hi):
    return lo + hi


def _psum(x, axis, n):
    if _pow2(n):
        return _allreduce(x, axis, n, _add)
    return lax.psum(x, axis)


def _gather(x, axis, n):
    if _pow2(n):
        return _allgather(x, axis, n)
    return lax.all_gather(x, axis, axis=0, tiled=False)


def _softmax_merge(lo, hi):
    peak = jnp.maximum(lo[0], hi[0])
    total = lo[1] * jnp.exp(lo[0] - peak) + hi[1] * jnp.exp(hi[0] - peak)
    return jnp.stack([peak, total, lo[2] + hi[2]])


def body(
    hidden,
    positions,
    counts,
    targets,
    dense_weight,
    dense_bias,
    norm_gain,
    norm_shift,
    embedding,
    decoder_bias,
):
    ways = lax.axis_size("vocab")
    groups = lax.axis_size("dp")
    model = hidden.shape[1]
    slots = positions.shape[1]
    group_rows = MEAN * ways
    total_rows = groups * group_rows
    in_block = dense_weight.shape[0]
    picked = jnp.take(hidden, positions[0], axis=0)
    listed_rows = lax.all_gather(picked, "vocab", axis=0, tiled=True)
    listed_ints = lax.all_gather(
        jnp.concatenate([counts, targets[0]]), "vocab", axis=0, tiled=False
    )
    listed_counts = listed_ints[:, 0]
    listed_tgt = listed_ints[:, 1:].reshape(-1)
    slot_ids = jnp.tile(jnp.arange(slots, dtype=jnp.int32), ways)
    count_of = jnp.repeat(listed_counts, slots)
    start_of = jnp.repeat(jnp.cumsum(listed_counts) - listed_counts, slots)
    valid = slot_ids < count_of
    dest = start_of + slot_ids
    chooser = (dest[None, :] == jnp.arange(group_rows, dtype=jnp.int32)[:, None]) & valid[None, :]
    rows = jnp.dot(
        chooser.astype(jnp.bfloat16), listed_rows, preferred_element_type=jnp.float32
    ).astype(jnp.bfloat16)
    tgt = jnp.sum(jnp.where(chooser, listed_tgt[None, :], 0), axis=1).astype(jnp.int32)
    blocks = rows.reshape(group_rows, groups, in_block).transpose(1, 0, 2)
    rows_in = lax.all_to_all(blocks, "dp", 0, 0, tiled=True).reshape(total_rows, in_block)
    tgt_all = _gather(tgt, "dp", groups).reshape(total_rows)
    part = jnp.dot(rows_in, dense_weight, preferred_element_type=jnp.float32)
    act = _psum(part, "dp", groups)
    act = jax.nn.gelu(act + dense_bias, approximate=False)
    stats = _psum(jnp.stack([jnp.sum(act, axis=1), jnp.sum(act * act, axis=1)]), "vocab", ways)
    mean = stats[0] / model
    var = stats[1] / model - mean * mean
    head_cols = (
        (act - mean[:, None]) * lax.rsqrt(var + EPS)[:, None] * norm_gain + norm_shift
    ).astype(jnp.bfloat16)
    head_all = _gather(head_cols, "vocab", ways).transpose(1, 0, 2).reshape(total_rows, model)
    vocab_rows = embedding.shape[0]
    first_id = (lax.axis_index("dp") * ways + lax.axis_index("vocab")) * vocab_rows
    ids = first_id + jnp.arange(vocab_rows, dtype=jnp.int32)
    logits = (
        jnp.einsum("rd,vd->rv", head_all, embedding, preferred_element_type=jnp.float32)
        + decoder_bias[None, :]
    )
    hit = tgt_all[:, None] == ids[None, :]
    row_max = jnp.max(logits, axis=1)
    local = jnp.stack(
        [
            row_max,
            jnp.sum(jnp.exp(logits - row_max[:, None]), axis=1),
            jnp.sum(jnp.where(hit, logits, 0.0), axis=1),
        ]
    )
    if _pow2(ways) and _pow2(groups):
        merged = _allreduce(_allreduce(local, "vocab", ways, _softmax_merge), "dp", groups, _softmax_merge)
        peak, denom, target_logit = merged[0], merged[1], merged[2]
    else:
        peak = lax.pmax(row_max, ("dp", "vocab"))
        denom, target_logit = lax.psum(
            (jnp.sum(jnp.exp(logits - peak[:, None]), axis=1), local[2]), ("dp", "vocab")
        )
    lse = peak + jnp.log(denom)
    row_loss = lse - target_logit
    diff = jnp.exp(logits - lse[:, None]) - hit.astype(jnp.float32)
    grad = (diff / total_rows).astype(jnp.bfloat16)
    emb_grad = jnp.einsum("rv,rd->vd", grad, head_all, preferred_element_type=jnp.float32).astype(
        jnp.bfloat16
    )
    bias_grad = jnp.sum(diff, axis=0) / total_rows
    return (emb_grad, bias_grad, row_loss)


def solution(mesh):
    return jax.shard_map(
        body,
        mesh=mesh,
        in_specs=(
            P(("dp", "vocab"), None),
            P(("dp", "vocab"), None),
            P(("dp", "vocab")),
            P(("dp", "vocab"), None),
            P("dp", "vocab"),
            P("vocab"),
            P("vocab"),
            P("vocab"),
            P(("dp", "vocab"), None),
            P(("dp", "vocab")),
        ),
        out_specs=(P(("dp", "vocab"), None), P(("dp", "vocab")), P()),
        check_vma=False,
    )
```

```python
import jax
import jax.numpy as jnp
from jax import lax
from jax.sharding import PartitionSpec as P

MEAN = 2


EPS = 1e-05


def _pow2(n):
    return n & (n - 1) == 0


def _canon(axis, step, mine, theirs):
    upper = (lax.axis_index(axis) & step) != 0
    return jnp.where(upper, theirs, mine), jnp.where(upper, mine, theirs)


def _allreduce(x, axis, n, merge):
    step = 1
    while step < n:
        theirs = lax.ppermute(x, axis, [(a, a ^ step) for a in range(n)])
        lo, hi = _canon(axis, step, x, theirs)
        x = merge(lo, hi)
        step *= 2
    return x


def _allgather(x, axis, n):
    buf = x[None]
    step = 1
    while step < n:
        theirs = lax.ppermute(buf, axis, [(a, a ^ step) for a in range(n)])
        upper = (lax.axis_index(axis) & step) != 0
        buf = jnp.where(upper, jnp.concatenate([theirs, buf]), jnp.concatenate([buf, theirs]))
        step *= 2
    return buf


def _reduce_scatter(x, axis, n):
    idx = lax.axis_index(axis)
    step = n // 2
    while step >= 1:
        halves = x.reshape((2, x.shape[0] // 2) + x.shape[1:])
        upper = (idx & step) != 0
        kept = jnp.where(upper, halves[1], halves[0])
        sent = jnp.where(upper, halves[0], halves[1])
        theirs = lax.ppermute(sent, axis, [(a, a ^ step) for a in range(n)])
        lo, hi = _canon(axis, step, kept, theirs)
        x = lo + hi
        step //= 2
    return x[0]


def _add(lo, hi):
    return lo + hi


def _psum(x, axis, n):
    if _pow2(n):
        return _allreduce(x, axis, n, _add)
    return lax.psum(x, axis)


def _gather(x, axis, n):
    if _pow2(n):
        return _allgather(x, axis, n)
    return lax.all_gather(x, axis, axis=0, tiled=False)


def _softmax_merge(lo, hi):
    peak = jnp.maximum(lo[0], hi[0])
    total = lo[1] * jnp.exp(lo[0] - peak) + hi[1] * jnp.exp(hi[0] - peak)
    return jnp.stack([peak, total, lo[2] + hi[2]])


def body(
    hidden,
    positions,
    counts,
    targets,
    dense_weight,
    dense_bias,
    norm_gain,
    norm_shift,
    embedding,
    decoder_bias,
):
    ways = lax.axis_size("vocab")
    groups = lax.axis_size("dp")
    model = hidden.shape[1]
    slots = positions.shape[1]
    group_rows = MEAN * ways
    total_rows = groups * group_rows
    in_block = dense_weight.shape[0]
    tokens = hidden.shape[0]
    onehot = (positions[0][:, None] == jnp.arange(tokens, dtype=jnp.int32)[None, :]).astype(hidden.dtype)
    picked = jnp.dot(onehot, hidden, preferred_element_type=jnp.float32).astype(hidden.dtype)
    count_row = jnp.broadcast_to(counts.astype(hidden.dtype)[:, None], (1, model))
    listed = lax.all_gather(jnp.concatenate([picked, count_row]), "vocab", axis=0, tiled=False)
    listed_rows = listed[:, :slots].reshape(ways * slots, model)
    listed_counts = listed[:, slots, 0].astype(jnp.int32)
    slot_ids = jnp.tile(jnp.arange(slots, dtype=jnp.int32), ways)
    row_ids = jnp.arange(group_rows, dtype=jnp.int32)

    def choose(group_counts):
        count_of = jnp.repeat(group_counts, slots)
        start_of = jnp.repeat(jnp.cumsum(group_counts) - group_counts, slots)
        valid = slot_ids < count_of
        dest = start_of + slot_ids
        return (dest[None, :] == row_ids[:, None]) & valid[None, :]

    chooser = choose(listed_counts)
    rows = jnp.dot(
        chooser.astype(jnp.bfloat16), listed_rows, preferred_element_type=jnp.float32
    ).astype(jnp.bfloat16)
    ints = jnp.concatenate([counts, targets[0]])
    all_ints = _gather(_gather(ints, "vocab", ways), "dp", groups).reshape(groups, ways, slots + 1)
    all_choosers = jax.vmap(choose)(all_ints[:, :, 0])
    tgt_all = jnp.sum(
        jnp.where(all_choosers, all_ints[:, None, :, 1:].reshape(groups, 1, ways * slots), 0), axis=2
    ).reshape(total_rows).astype(jnp.int32)
    blocks = rows.reshape(group_rows, groups, in_block).transpose(1, 0, 2)
    rows_in = lax.all_to_all(blocks, "dp", 0, 0, tiled=True).reshape(total_rows, in_block)
    part = jnp.dot(rows_in, dense_weight, preferred_element_type=jnp.float32)
    if _pow2(groups):
        act = _reduce_scatter(part.reshape(groups, group_rows, -1), "dp", groups)
    else:
        act = lax.psum_scatter(part.reshape(groups, group_rows, -1), "dp", scatter_dimension=0, tiled=True)[0]
    act = jax.nn.gelu(act + dense_bias, approximate=False)
    stats = _psum(jnp.stack([jnp.sum(act, axis=1), jnp.sum(act * act, axis=1)]), "vocab", ways)
    mean = stats[0] / model
    var = stats[1] / model - mean * mean
    head_rows = (
        (act - mean[:, None]) * lax.rsqrt(var + EPS)[:, None] * norm_gain + norm_shift
    ).astype(jnp.bfloat16)
    head_cols = _gather(head_rows, "dp", groups).reshape(total_rows, -1)
    head_all = _gather(head_cols, "vocab", ways).transpose(1, 0, 2).reshape(total_rows, model)
    vocab_rows = embedding.shape[0]
    first_id = (lax.axis_index("dp") * ways + lax.axis_index("vocab")) * vocab_rows
    ids = first_id + jnp.arange(vocab_rows, dtype=jnp.int32)
    logits = (
        jnp.einsum("rd,vd->rv", head_all, embedding, preferred_element_type=jnp.float32)
        + decoder_bias[None, :]
    )
    hit = tgt_all[:, None] == ids[None, :]
    row_max = jnp.max(logits, axis=1)
    local = jnp.stack(
        [
            row_max,
            jnp.sum(jnp.exp(logits - row_max[:, None]), axis=1),
            jnp.sum(jnp.where(hit, logits, 0.0), axis=1),
        ]
    )
    if _pow2(ways) and _pow2(groups):
        merged = _allreduce(_allreduce(local, "vocab", ways, _softmax_merge), "dp", groups, _softmax_merge)
        peak, denom, target_logit = merged[0], merged[1], merged[2]
    else:
        peak = lax.pmax(row_max, ("dp", "vocab"))
        denom, target_logit = lax.psum(
            (jnp.sum(jnp.exp(logits - peak[:, None]), axis=1), local[2]), ("dp", "vocab")
        )
    lse = peak + jnp.log(denom)
    row_loss = lse - target_logit
    diff = jnp.exp(logits - lse[:, None]) - hit.astype(jnp.float32)
    grad = (diff / total_rows).astype(jnp.bfloat16)
    emb_grad = jnp.einsum("rv,rd->vd", grad, head_all, preferred_element_type=jnp.float32).astype(
        jnp.bfloat16
    )
    bias_grad = jnp.sum(diff, axis=0) / total_rows
    return (emb_grad, bias_grad, row_loss)


def solution(mesh):
    return jax.shard_map(
        body,
        mesh=mesh,
        in_specs=(
            P(("dp", "vocab"), None),
            P(("dp", "vocab"), None),
            P(("dp", "vocab")),
            P(("dp", "vocab"), None),
            P("dp", "vocab"),
            P("vocab"),
            P("vocab"),
            P("vocab"),
            P(("dp", "vocab"), None),
            P(("dp", "vocab")),
        ),
        out_specs=(P(("dp", "vocab"), None), P(("dp", "vocab")), P()),
        check_vma=False,
    )
```

```python
import jax
import jax.numpy as jnp
from jax import lax
from jax.sharding import PartitionSpec as P

MEAN = 2


EPS = 1e-05


def _pow2(n):
    return n & (n - 1) == 0


def _canon(axis, step, mine, theirs):
    upper = (lax.axis_index(axis) & step) != 0
    return jnp.where(upper, theirs, mine), jnp.where(upper, mine, theirs)


def _allreduce(x, axis, n, merge):
    step = 1
    while step < n:
        theirs = lax.ppermute(x, axis, [(a, a ^ step) for a in range(n)])
        lo, hi = _canon(axis, step, x, theirs)
        x = merge(lo, hi)
        step *= 2
    return x


def _allgather(x, axis, n, order=None):
    order = order or _steps(n)
    buf = x[None]
    for step in order:
        theirs = lax.ppermute(buf, axis, [(a, a ^ step) for a in range(n)])
        upper = (lax.axis_index(axis) & step) != 0
        buf = jnp.where(upper, jnp.concatenate([theirs, buf]), jnp.concatenate([buf, theirs]))
    block_of = [sum(((p >> t) & 1) * step for t, step in enumerate(order)) for p in range(n)]
    if block_of != list(range(n)):
        place = [block_of.index(k) for k in range(n)]
        buf = buf[jnp.array(place, dtype=jnp.int32)]
    return buf


def _steps(n):
    out, step = [], 1
    while step < n:
        out.append(step)
        step *= 2
    return out


def _reduce_scatter(x, axis, n, order=None):
    order = order or _steps(n)[::-1]
    idx = lax.axis_index(axis)
    bits = _steps(n)[::-1]
    rest = x.shape[1:]
    x = x.reshape((2,) * len(bits) + rest)
    for step in order:
        at = bits.index(step)
        upper = (idx & step) != 0
        low, high = jnp.take(x, 0, axis=at), jnp.take(x, 1, axis=at)
        kept = jnp.where(upper, high, low)
        sent = jnp.where(upper, low, high)
        theirs = lax.ppermute(sent, axis, [(a, a ^ step) for a in range(n)])
        lo, hi = _canon(axis, step, kept, theirs)
        x = lo + hi
        bits.pop(at)
    return x


def _pieces(t):
    return jnp.concatenate([t >> 16, (t >> 8) & 255, t & 255])


def _unpieces(p):
    return p[..., 0, :] * 65536 + p[..., 1, :] * 256 + p[..., 2, :]


def _add(lo, hi):
    return lo + hi


def _psum(x, axis, n):
    if _pow2(n):
        return _allreduce(x, axis, n, _add)
    return lax.psum(x, axis)


def _gather(x, axis, n, order=None):
    if _pow2(n):
        return _allgather(x, axis, n, order)
    return lax.all_gather(x, axis, axis=0, tiled=False)


def _softmax_merge(lo, hi):
    peak = jnp.maximum(lo[0], hi[0])
    total = lo[1] * jnp.exp(lo[0] - peak) + hi[1] * jnp.exp(hi[0] - peak)
    return jnp.stack([peak, total, lo[2] + hi[2]])


def body(
    hidden,
    positions,
    counts,
    targets,
    dense_weight,
    dense_bias,
    norm_gain,
    norm_shift,
    embedding,
    decoder_bias,
):
    ways = lax.axis_size("vocab")
    groups = lax.axis_size("dp")
    model = hidden.shape[1]
    slots = positions.shape[1]
    group_rows = MEAN * ways
    total_rows = groups * group_rows
    in_block = dense_weight.shape[0]
    tokens = hidden.shape[0]
    onehot = (positions[0][:, None] == jnp.arange(tokens, dtype=jnp.int32)[None, :]).astype(hidden.dtype)
    picked = jnp.dot(onehot, hidden, preferred_element_type=jnp.float32).astype(hidden.dtype)
    meta = jnp.zeros((1, model), jnp.int32)
    meta = meta.at[0, 0].set(counts[0])
    meta = lax.dynamic_update_slice(meta, _pieces(targets[0])[None], (0, 1))
    listed = lax.all_gather(
        jnp.concatenate([picked, meta.astype(hidden.dtype)]), "vocab", axis=0, tiled=False
    )
    listed_rows = listed[:, :slots].reshape(ways * slots, model)
    listed_meta = listed[:, slots, : 1 + 3 * slots].astype(jnp.int32)
    listed_counts = listed_meta[:, 0]
    listed_tgt = _unpieces(listed_meta[:, 1:].reshape(ways, 3, slots)).reshape(ways * slots)
    slot_ids = jnp.tile(jnp.arange(slots, dtype=jnp.int32), ways)
    row_ids = jnp.arange(group_rows, dtype=jnp.int32)

    def choose(group_counts):
        count_of = jnp.repeat(group_counts, slots)
        start_of = jnp.repeat(jnp.cumsum(group_counts) - group_counts, slots)
        valid = slot_ids < count_of
        dest = start_of + slot_ids
        return (dest[None, :] == row_ids[:, None]) & valid[None, :]

    chooser = choose(listed_counts)
    rows = jnp.dot(
        chooser.astype(jnp.bfloat16), listed_rows, preferred_element_type=jnp.float32
    ).astype(jnp.bfloat16)
    tgt = jnp.sum(jnp.where(chooser, listed_tgt[None, :], 0), axis=1).astype(jnp.int32)
    blocks = rows.reshape(group_rows, groups, in_block).transpose(1, 0, 2)
    tgt_row = jnp.zeros((in_block,), jnp.int32).at[: 3 * group_rows].set(_pieces(tgt))
    tgt_rows = jnp.broadcast_to(tgt_row.astype(jnp.bfloat16), (groups, 1, in_block))
    got = lax.all_to_all(jnp.concatenate([blocks, tgt_rows], axis=1), "dp", 0, 0, tiled=True)
    rows_in = got[:, :group_rows].reshape(total_rows, in_block)
    tgt_all = _unpieces(
        got[:, group_rows, : 3 * group_rows].astype(jnp.int32).reshape(groups, 3, group_rows)
    ).reshape(total_rows)
    part = jnp.dot(rows_in, dense_weight, preferred_element_type=jnp.float32)
    if _pow2(groups):
        act = _reduce_scatter(part.reshape(groups, group_rows, -1), "dp", groups, _steps(groups))
    else:
        act = lax.psum_scatter(part.reshape(groups, group_rows, -1), "dp", scatter_dimension=0, tiled=True)[0]
    act = jax.nn.gelu(act + dense_bias, approximate=False)
    stats = _psum(jnp.stack([jnp.sum(act, axis=1), jnp.sum(act * act, axis=1)]), "vocab", ways)
    mean = stats[0] / model
    var = stats[1] / model - mean * mean
    head_rows = (
        (act - mean[:, None]) * lax.rsqrt(var + EPS)[:, None] * norm_gain + norm_shift
    ).astype(jnp.bfloat16)
    head_cols = _gather(head_rows, "dp", groups, _steps(groups)[::-1]).reshape(total_rows, -1)
    head_all = _gather(head_cols, "vocab", ways, _steps(ways)[::-1]).transpose(1, 0, 2).reshape(total_rows, model)
    vocab_rows = embedding.shape[0]
    first_id = (lax.axis_index("dp") * ways + lax.axis_index("vocab")) * vocab_rows
    ids = first_id + jnp.arange(vocab_rows, dtype=jnp.int32)
    logits = (
        jnp.einsum("rd,vd->rv", head_all, embedding, preferred_element_type=jnp.float32)
        + decoder_bias[None, :]
    )
    hit = tgt_all[:, None] == ids[None, :]
    row_max = jnp.max(logits, axis=1)
    local = jnp.stack(
        [
            row_max,
            jnp.sum(jnp.exp(logits - row_max[:, None]), axis=1),
            jnp.sum(jnp.where(hit, logits, 0.0), axis=1),
        ]
    )
    if _pow2(ways) and _pow2(groups):
        merged = _allreduce(_allreduce(local, "vocab", ways, _softmax_merge), "dp", groups, _softmax_merge)
        peak, denom, target_logit = merged[0], merged[1], merged[2]
    else:
        peak = lax.pmax(row_max, ("dp", "vocab"))
        denom, target_logit = lax.psum(
            (jnp.sum(jnp.exp(logits - peak[:, None]), axis=1), local[2]), ("dp", "vocab")
        )
    lse = peak + jnp.log(denom)
    row_loss = lse - target_logit
    diff = jnp.exp(logits - lse[:, None]) - hit.astype(jnp.float32)
    grad = (diff / total_rows).astype(jnp.bfloat16)
    emb_grad = jnp.einsum("rv,rd->vd", grad, head_all, preferred_element_type=jnp.float32).astype(
        jnp.bfloat16
    )
    bias_grad = jnp.sum(diff, axis=0) / total_rows
    return (emb_grad, bias_grad, row_loss)


def solution(mesh):
    return jax.shard_map(
        body,
        mesh=mesh,
        in_specs=(
            P(("dp", "vocab"), None),
            P(("dp", "vocab"), None),
            P(("dp", "vocab")),
            P(("dp", "vocab"), None),
            P("dp", "vocab"),
            P("vocab"),
            P("vocab"),
            P("vocab"),
            P(("dp", "vocab"), None),
            P(("dp", "vocab")),
        ),
        out_specs=(P(("dp", "vocab"), None), P(("dp", "vocab")), P()),
        check_vma=False,
    )
```

```python
import jax
import jax.numpy as jnp
from jax import lax
from jax.sharding import PartitionSpec as P

MEAN = 2


EPS = 1e-05


def _pow2(n):
    return n & (n - 1) == 0


def _canon(axis, step, mine, theirs):
    upper = (lax.axis_index(axis) & step) != 0
    return jnp.where(upper, theirs, mine), jnp.where(upper, mine, theirs)


def _allreduce(x, axis, n, merge):
    step = 1
    while step < n:
        theirs = lax.ppermute(x, axis, [(a, a ^ step) for a in range(n)])
        lo, hi = _canon(axis, step, x, theirs)
        x = merge(lo, hi)
        step *= 2
    return x


def _allgather(x, axis, n, order=None):
    order = order or _steps(n)
    buf = x[None]
    for step in order:
        theirs = lax.ppermute(buf, axis, [(a, a ^ step) for a in range(n)])
        upper = (lax.axis_index(axis) & step) != 0
        buf = jnp.where(upper, jnp.concatenate([theirs, buf]), jnp.concatenate([buf, theirs]))
    block_of = [sum(((p >> t) & 1) * step for t, step in enumerate(order)) for p in range(n)]
    if block_of != list(range(n)):
        place = [block_of.index(k) for k in range(n)]
        buf = buf[jnp.array(place, dtype=jnp.int32)]
    return buf


def _steps(n):
    out, step = [], 1
    while step < n:
        out.append(step)
        step *= 2
    return out


def _reduce_scatter(x, axis, n, order=None):
    order = order or _steps(n)[::-1]
    idx = lax.axis_index(axis)
    bits = _steps(n)[::-1]
    rest = x.shape[1:]
    x = x.reshape((2,) * len(bits) + rest)
    for step in order:
        at = bits.index(step)
        upper = (idx & step) != 0
        low, high = jnp.take(x, 0, axis=at), jnp.take(x, 1, axis=at)
        kept = jnp.where(upper, high, low)
        sent = jnp.where(upper, low, high)
        theirs = lax.ppermute(sent, axis, [(a, a ^ step) for a in range(n)])
        lo, hi = _canon(axis, step, kept, theirs)
        x = lo + hi
        bits.pop(at)
    return x


def _pieces(t):
    return jnp.concatenate([t >> 16, (t >> 8) & 255, t & 255])


def _unpieces(p):
    return p[..., 0, :] * 65536 + p[..., 1, :] * 256 + p[..., 2, :]


def _add(lo, hi):
    return lo + hi


def _psum(x, axis, n):
    if _pow2(n):
        return _allreduce(x, axis, n, _add)
    return lax.psum(x, axis)


def _gather(x, axis, n, order=None):
    if _pow2(n):
        return _allgather(x, axis, n, order)
    return lax.all_gather(x, axis, axis=0, tiled=False)


def _softmax_merge(lo, hi):
    peak = jnp.maximum(lo[0], hi[0])
    total = lo[1] * jnp.exp(lo[0] - peak) + hi[1] * jnp.exp(hi[0] - peak)
    return jnp.stack([peak, total, lo[2] + hi[2]])


def body(
    hidden,
    positions,
    counts,
    targets,
    dense_weight,
    dense_bias,
    norm_gain,
    norm_shift,
    embedding,
    decoder_bias,
):
    ways = lax.axis_size("vocab")
    groups = lax.axis_size("dp")
    model = hidden.shape[1]
    slots = positions.shape[1]
    group_rows = MEAN * ways
    total_rows = groups * group_rows
    in_block = dense_weight.shape[0]
    tokens = hidden.shape[0]
    onehot = (positions[0][:, None] == jnp.arange(tokens, dtype=jnp.int32)[None, :]).astype(hidden.dtype)
    picked = jnp.dot(onehot, hidden, preferred_element_type=jnp.float32).astype(hidden.dtype)
    meta = jnp.zeros((in_block,), jnp.int32).at[0].set(counts[0])
    meta = lax.dynamic_update_slice(meta, _pieces(targets[0]), (1,))
    blocks = jnp.concatenate(
        [
            picked.reshape(slots, groups, in_block).transpose(1, 0, 2),
            jnp.broadcast_to(meta.astype(hidden.dtype), (groups, 1, in_block)),
        ],
        axis=1,
    )
    got = lax.all_to_all(jnp.repeat(blocks, ways, axis=0), ("dp", "vocab"), 0, 0, tiled=True)
    got = got.reshape(groups, ways, slots + 1, in_block)
    slot_rows = got[:, :, :slots].reshape(groups, ways * slots, in_block)
    got_meta = got[:, :, slots, : 1 + 3 * slots].astype(jnp.int32)
    got_tgt = _unpieces(got_meta[:, :, 1:].reshape(groups, ways, 3, slots)).reshape(groups, ways * slots)
    slot_ids = jnp.tile(jnp.arange(slots, dtype=jnp.int32), ways)
    row_ids = jnp.arange(group_rows, dtype=jnp.int32)

    def choose(group_counts):
        count_of = jnp.repeat(group_counts, slots)
        start_of = jnp.repeat(jnp.cumsum(group_counts) - group_counts, slots)
        valid = slot_ids < count_of
        dest = start_of + slot_ids
        return (dest[None, :] == row_ids[:, None]) & valid[None, :]

    choosers = jax.vmap(choose)(got_meta[:, :, 0])
    rows_in = jnp.einsum(
        "grs,gsd->grd", choosers.astype(hidden.dtype), slot_rows, preferred_element_type=jnp.float32
    ).astype(hidden.dtype).reshape(total_rows, in_block)
    tgt_all = jnp.sum(jnp.where(choosers, got_tgt[:, None, :], 0), axis=2).reshape(total_rows)
    part = jnp.dot(rows_in, dense_weight, preferred_element_type=jnp.float32)
    if _pow2(groups):
        act = _reduce_scatter(part.reshape(groups, group_rows, -1), "dp", groups, _steps(groups))
    else:
        act = lax.psum_scatter(part.reshape(groups, group_rows, -1), "dp", scatter_dimension=0, tiled=True)[0]
    act = jax.nn.gelu(act + dense_bias, approximate=False)
    stats = _psum(jnp.stack([jnp.sum(act, axis=1), jnp.sum(act * act, axis=1)]), "vocab", ways)
    mean = stats[0] / model
    var = stats[1] / model - mean * mean
    head_rows = (
        (act - mean[:, None]) * lax.rsqrt(var + EPS)[:, None] * norm_gain + norm_shift
    ).astype(jnp.bfloat16)
    head_cols = _gather(head_rows, "dp", groups, _steps(groups)[::-1]).reshape(total_rows, -1)
    head_all = _gather(head_cols, "vocab", ways, _steps(ways)[::-1]).transpose(1, 0, 2).reshape(total_rows, model)
    vocab_rows = embedding.shape[0]
    first_id = (lax.axis_index("dp") * ways + lax.axis_index("vocab")) * vocab_rows
    ids = first_id + jnp.arange(vocab_rows, dtype=jnp.int32)
    logits = (
        jnp.einsum("rd,vd->rv", head_all, embedding, preferred_element_type=jnp.float32)
        + decoder_bias[None, :]
    )
    hit = tgt_all[:, None] == ids[None, :]
    row_max = jnp.max(logits, axis=1)
    local = jnp.stack(
        [
            row_max,
            jnp.sum(jnp.exp(logits - row_max[:, None]), axis=1),
            jnp.sum(jnp.where(hit, logits, 0.0), axis=1),
        ]
    )
    devices = groups * ways
    every = lax.all_to_all(jnp.broadcast_to(local[None], (devices,) + local.shape), ("dp", "vocab"), 0, 0, tiled=True)
    peak = jnp.max(every[:, 0], axis=0)
    denom = jnp.sum(every[:, 1] * jnp.exp(every[:, 0] - peak[None, :]), axis=0)
    target_logit = jnp.sum(every[:, 2], axis=0)
    lse = peak + jnp.log(denom)
    row_loss = lse - target_logit
    diff = jnp.exp(logits - lse[:, None]) - hit.astype(jnp.float32)
    grad = (diff / total_rows).astype(jnp.bfloat16)
    emb_grad = jnp.einsum("rv,rd->vd", grad, head_all, preferred_element_type=jnp.float32).astype(
        jnp.bfloat16
    )
    bias_grad = jnp.sum(diff, axis=0) / total_rows
    return (emb_grad, bias_grad, row_loss)


def solution(mesh):
    return jax.shard_map(
        body,
        mesh=mesh,
        in_specs=(
            P(("dp", "vocab"), None),
            P(("dp", "vocab"), None),
            P(("dp", "vocab")),
            P(("dp", "vocab"), None),
            P("dp", "vocab"),
            P("vocab"),
            P("vocab"),
            P("vocab"),
            P(("dp", "vocab"), None),
            P(("dp", "vocab")),
        ),
        out_specs=(P(("dp", "vocab"), None), P(("dp", "vocab")), P()),
        check_vma=False,
    )
```

```python
import jax
import jax.numpy as jnp
from jax import lax
from jax.sharding import PartitionSpec as P

MEAN = 2


EPS = 1e-05


def _pow2(n):
    return n & (n - 1) == 0


def _canon(axis, step, mine, theirs):
    upper = (lax.axis_index(axis) & step) != 0
    return jnp.where(upper, theirs, mine), jnp.where(upper, mine, theirs)


def _allreduce(x, axis, n, merge):
    step = 1
    while step < n:
        theirs = lax.ppermute(x, axis, [(a, a ^ step) for a in range(n)])
        lo, hi = _canon(axis, step, x, theirs)
        x = merge(lo, hi)
        step *= 2
    return x


def _allgather(x, axis, n, order=None):
    order = order or _steps(n)
    buf = x[None]
    for step in order:
        theirs = lax.ppermute(buf, axis, [(a, a ^ step) for a in range(n)])
        upper = (lax.axis_index(axis) & step) != 0
        buf = jnp.where(upper, jnp.concatenate([theirs, buf]), jnp.concatenate([buf, theirs]))
    block_of = [sum(((p >> t) & 1) * step for t, step in enumerate(order)) for p in range(n)]
    if block_of != list(range(n)):
        place = [block_of.index(k) for k in range(n)]
        buf = buf[jnp.array(place, dtype=jnp.int32)]
    return buf


def _steps(n):
    out, step = [], 1
    while step < n:
        out.append(step)
        step *= 2
    return out


def _reduce_scatter(x, axis, n, order=None):
    order = order or _steps(n)[::-1]
    idx = lax.axis_index(axis)
    bits = _steps(n)[::-1]
    rest = x.shape[1:]
    x = x.reshape((2,) * len(bits) + rest)
    for step in order:
        at = bits.index(step)
        upper = (idx & step) != 0
        low, high = jnp.take(x, 0, axis=at), jnp.take(x, 1, axis=at)
        kept = jnp.where(upper, high, low)
        sent = jnp.where(upper, low, high)
        theirs = lax.ppermute(sent, axis, [(a, a ^ step) for a in range(n)])
        lo, hi = _canon(axis, step, kept, theirs)
        x = lo + hi
        bits.pop(at)
    return x


def _pieces(t):
    return jnp.concatenate([t >> 16, (t >> 8) & 255, t & 255])


def _unpieces(p):
    return p[..., 0, :] * 65536 + p[..., 1, :] * 256 + p[..., 2, :]


def _add(lo, hi):
    return lo + hi


def _psum(x, axis, n):
    if _pow2(n):
        return _allreduce(x, axis, n, _add)
    return lax.psum(x, axis)


def _gather(x, axis, n, order=None):
    if _pow2(n):
        return _allgather(x, axis, n, order)
    return lax.all_gather(x, axis, axis=0, tiled=False)


def _softmax_merge(lo, hi):
    peak = jnp.maximum(lo[0], hi[0])
    total = lo[1] * jnp.exp(lo[0] - peak) + hi[1] * jnp.exp(hi[0] - peak)
    return jnp.stack([peak, total, lo[2] + hi[2]])


def body(
    hidden,
    positions,
    counts,
    targets,
    dense_weight,
    dense_bias,
    norm_gain,
    norm_shift,
    embedding,
    decoder_bias,
):
    ways = lax.axis_size("vocab")
    groups = lax.axis_size("dp")
    model = hidden.shape[1]
    slots = positions.shape[1]
    group_rows = MEAN * ways
    total_rows = groups * group_rows
    in_block = dense_weight.shape[0]
    tokens = hidden.shape[0]
    onehot = (positions[0][:, None] == jnp.arange(tokens, dtype=jnp.int32)[None, :]).astype(hidden.dtype)
    picked = jnp.dot(onehot, hidden, preferred_element_type=jnp.float32).astype(hidden.dtype)
    meta = jnp.zeros((in_block,), jnp.int32).at[0].set(counts[0])
    meta = lax.dynamic_update_slice(meta, _pieces(targets[0]), (1,))
    blocks = jnp.concatenate(
        [
            picked.reshape(slots, groups, in_block).transpose(1, 0, 2),
            jnp.broadcast_to(meta.astype(hidden.dtype), (groups, 1, in_block)),
        ],
        axis=1,
    )
    got = lax.all_to_all(jnp.repeat(blocks, ways, axis=0), ("dp", "vocab"), 0, 0, tiled=True)
    got = got.reshape(groups, ways, slots + 1, in_block)
    slot_rows = got[:, :, :slots].reshape(groups, ways * slots, in_block)
    got_meta = got[:, :, slots, : 1 + 3 * slots].astype(jnp.int32)
    got_tgt = _unpieces(got_meta[:, :, 1:].reshape(groups, ways, 3, slots)).reshape(groups, ways * slots)
    slot_ids = jnp.tile(jnp.arange(slots, dtype=jnp.int32), ways)
    row_ids = jnp.arange(group_rows, dtype=jnp.int32)

    def choose(group_counts):
        count_of = jnp.repeat(group_counts, slots)
        start_of = jnp.repeat(jnp.cumsum(group_counts) - group_counts, slots)
        valid = slot_ids < count_of
        dest = start_of + slot_ids
        return (dest[None, :] == row_ids[:, None]) & valid[None, :]

    choosers = jax.vmap(choose)(got_meta[:, :, 0])
    rows_in = jnp.einsum(
        "grs,gsd->grd", choosers.astype(hidden.dtype), slot_rows, preferred_element_type=jnp.float32
    ).astype(hidden.dtype).reshape(total_rows, in_block)
    tgt_all = jnp.sum(jnp.where(choosers, got_tgt[:, None, :], 0), axis=2).reshape(total_rows)
    part = jnp.dot(rows_in, dense_weight, preferred_element_type=jnp.float32)
    act = jnp.sum(lax.all_to_all(part.reshape(groups, group_rows, -1), "dp", 0, 0, tiled=True), axis=0)
    act = jax.nn.gelu(act + dense_bias, approximate=False)
    stats = _psum(jnp.stack([jnp.sum(act, axis=1), jnp.sum(act * act, axis=1)]), "vocab", ways)
    mean = stats[0] / model
    var = stats[1] / model - mean * mean
    head_rows = (
        (act - mean[:, None]) * lax.rsqrt(var + EPS)[:, None] * norm_gain + norm_shift
    ).astype(jnp.bfloat16)
    devices = groups * ways
    every_head = lax.all_to_all(
        jnp.broadcast_to(head_rows[None], (devices,) + head_rows.shape), ("dp", "vocab"), 0, 0, tiled=True
    )
    head_all = every_head.reshape(groups, ways, group_rows, -1).transpose(0, 2, 1, 3).reshape(total_rows, model)
    vocab_rows = embedding.shape[0]
    first_id = (lax.axis_index("dp") * ways + lax.axis_index("vocab")) * vocab_rows
    ids = first_id + jnp.arange(vocab_rows, dtype=jnp.int32)
    logits = (
        jnp.einsum("rd,vd->rv", head_all, embedding, preferred_element_type=jnp.float32)
        + decoder_bias[None, :]
    )
    hit = tgt_all[:, None] == ids[None, :]
    row_max = jnp.max(logits, axis=1)
    local = jnp.stack(
        [
            row_max,
            jnp.sum(jnp.exp(logits - row_max[:, None]), axis=1),
            jnp.sum(jnp.where(hit, logits, 0.0), axis=1),
        ]
    )
    every = lax.all_to_all(jnp.broadcast_to(local[None], (devices,) + local.shape), ("dp", "vocab"), 0, 0, tiled=True)
    peak = jnp.max(every[:, 0], axis=0)
    denom = jnp.sum(every[:, 1] * jnp.exp(every[:, 0] - peak[None, :]), axis=0)
    target_logit = jnp.sum(every[:, 2], axis=0)
    lse = peak + jnp.log(denom)
    row_loss = lse - target_logit
    diff = jnp.exp(logits - lse[:, None]) - hit.astype(jnp.float32)
    grad = (diff / total_rows).astype(jnp.bfloat16)
    emb_grad = jnp.einsum("rv,rd->vd", grad, head_all, preferred_element_type=jnp.float32).astype(
        jnp.bfloat16
    )
    bias_grad = jnp.sum(diff, axis=0) / total_rows
    return (emb_grad, bias_grad, row_loss)


def solution(mesh):
    return jax.shard_map(
        body,
        mesh=mesh,
        in_specs=(
            P(("dp", "vocab"), None),
            P(("dp", "vocab"), None),
            P(("dp", "vocab")),
            P(("dp", "vocab"), None),
            P("dp", "vocab"),
            P("vocab"),
            P("vocab"),
            P("vocab"),
            P(("dp", "vocab"), None),
            P(("dp", "vocab")),
        ),
        out_specs=(P(("dp", "vocab"), None), P(("dp", "vocab")), P()),
        check_vma=False,
    )
```

```python
import jax
import jax.numpy as jnp
from jax import lax
from jax.sharding import PartitionSpec as P

MEAN = 2


EPS = 1e-05


def _pow2(n):
    return n & (n - 1) == 0


def _canon(axis, step, mine, theirs):
    upper = (lax.axis_index(axis) & step) != 0
    return jnp.where(upper, theirs, mine), jnp.where(upper, mine, theirs)


def _allreduce(x, axis, n, merge):
    step = 1
    while step < n:
        theirs = lax.ppermute(x, axis, [(a, a ^ step) for a in range(n)])
        lo, hi = _canon(axis, step, x, theirs)
        x = merge(lo, hi)
        step *= 2
    return x


def _allgather(x, axis, n, order=None):
    order = order or _steps(n)
    buf = x[None]
    for step in order:
        theirs = lax.ppermute(buf, axis, [(a, a ^ step) for a in range(n)])
        upper = (lax.axis_index(axis) & step) != 0
        buf = jnp.where(upper, jnp.concatenate([theirs, buf]), jnp.concatenate([buf, theirs]))
    block_of = [sum(((p >> t) & 1) * step for t, step in enumerate(order)) for p in range(n)]
    if block_of != list(range(n)):
        place = [block_of.index(k) for k in range(n)]
        buf = buf[jnp.array(place, dtype=jnp.int32)]
    return buf


def _steps(n):
    out, step = [], 1
    while step < n:
        out.append(step)
        step *= 2
    return out


def _reduce_scatter(x, axis, n, order=None):
    order = order or _steps(n)[::-1]
    idx = lax.axis_index(axis)
    bits = _steps(n)[::-1]
    rest = x.shape[1:]
    x = x.reshape((2,) * len(bits) + rest)
    for step in order:
        at = bits.index(step)
        upper = (idx & step) != 0
        low, high = jnp.take(x, 0, axis=at), jnp.take(x, 1, axis=at)
        kept = jnp.where(upper, high, low)
        sent = jnp.where(upper, low, high)
        theirs = lax.ppermute(sent, axis, [(a, a ^ step) for a in range(n)])
        lo, hi = _canon(axis, step, kept, theirs)
        x = lo + hi
        bits.pop(at)
    return x


def _pieces(t):
    return jnp.concatenate([t >> 16, (t >> 8) & 255, t & 255])


def _unpieces(p):
    return p[..., 0, :] * 65536 + p[..., 1, :] * 256 + p[..., 2, :]


def _add(lo, hi):
    return lo + hi


def _psum(x, axis, n):
    if _pow2(n):
        return _allreduce(x, axis, n, _add)
    return lax.psum(x, axis)


def _gather(x, axis, n, order=None):
    if _pow2(n):
        return _allgather(x, axis, n, order)
    return lax.all_gather(x, axis, axis=0, tiled=False)


def _softmax_merge(lo, hi):
    peak = jnp.maximum(lo[0], hi[0])
    total = lo[1] * jnp.exp(lo[0] - peak) + hi[1] * jnp.exp(hi[0] - peak)
    return jnp.stack([peak, total, lo[2] + hi[2]])


def body(
    hidden,
    positions,
    counts,
    targets,
    dense_weight,
    dense_bias,
    norm_gain,
    norm_shift,
    embedding,
    decoder_bias,
):
    ways = lax.axis_size("vocab")
    groups = lax.axis_size("dp")
    model = hidden.shape[1]
    slots = positions.shape[1]
    group_rows = MEAN * ways
    total_rows = groups * group_rows
    in_block = dense_weight.shape[0]
    tokens = hidden.shape[0]
    onehot = (positions[0][:, None] == jnp.arange(tokens, dtype=jnp.int32)[None, :]).astype(hidden.dtype)
    picked = jnp.dot(onehot, hidden, preferred_element_type=jnp.float32).astype(hidden.dtype)
    meta = jnp.zeros((in_block,), jnp.int32).at[0].set(counts[0])
    meta = lax.dynamic_update_slice(meta, _pieces(targets[0]), (1,))
    blocks = jnp.concatenate(
        [
            picked.reshape(slots, groups, in_block).transpose(1, 0, 2),
            jnp.broadcast_to(meta.astype(hidden.dtype), (groups, 1, in_block)),
        ],
        axis=1,
    )
    got = lax.all_to_all(jnp.repeat(blocks, ways, axis=0), ("dp", "vocab"), 0, 0, tiled=True)
    got = got.reshape(groups, ways, slots + 1, in_block)
    slot_rows = got[:, :, :slots].reshape(groups, ways * slots, in_block)
    got_meta = got[:, :, slots, : 1 + 3 * slots].astype(jnp.int32)
    got_tgt = _unpieces(got_meta[:, :, 1:].reshape(groups, ways, 3, slots)).reshape(groups, ways * slots)
    slot_ids = jnp.tile(jnp.arange(slots, dtype=jnp.int32), ways)
    row_ids = jnp.arange(group_rows, dtype=jnp.int32)

    def choose(group_counts):
        count_of = jnp.repeat(group_counts, slots)
        start_of = jnp.repeat(jnp.cumsum(group_counts) - group_counts, slots)
        valid = slot_ids < count_of
        dest = start_of + slot_ids
        return (dest[None, :] == row_ids[:, None]) & valid[None, :]

    choosers = jax.vmap(choose)(got_meta[:, :, 0])
    rows_in = jnp.einsum(
        "grs,gsd->grd", choosers.astype(hidden.dtype), slot_rows, preferred_element_type=jnp.float32
    ).astype(hidden.dtype).reshape(total_rows, in_block)
    tgt_all = jnp.sum(jnp.where(choosers, got_tgt[:, None, :], 0), axis=2).reshape(total_rows)
    part = jnp.dot(rows_in, dense_weight, preferred_element_type=jnp.float32)
    act = jnp.sum(lax.all_to_all(part.reshape(groups, group_rows, -1), "dp", 0, 0, tiled=True), axis=0)
    act = jax.nn.gelu(act + dense_bias, approximate=False)
    pieces = _gather(jnp.concatenate([act, norm_gain[None], norm_shift[None]]), "vocab", ways, _steps(ways)[::-1])
    pieces = pieces.transpose(1, 0, 2).reshape(group_rows + 2, model)
    act, gain, shift = pieces[:group_rows], pieces[group_rows], pieces[group_rows + 1]
    mean = jnp.sum(act, axis=1) / model
    var = jnp.sum(act * act, axis=1) / model - mean * mean
    head_rows = ((act - mean[:, None]) * lax.rsqrt(var + EPS)[:, None] * gain + shift).astype(jnp.bfloat16)
    head_all = lax.all_to_all(
        jnp.broadcast_to(head_rows[None], (groups,) + head_rows.shape), "dp", 0, 0, tiled=True
    ).reshape(total_rows, model)
    devices = groups * ways
    vocab_rows = embedding.shape[0]
    first_id = (lax.axis_index("dp") * ways + lax.axis_index("vocab")) * vocab_rows
    ids = first_id + jnp.arange(vocab_rows, dtype=jnp.int32)
    logits = (
        jnp.einsum("rd,vd->rv", head_all, embedding, preferred_element_type=jnp.float32)
        + decoder_bias[None, :]
    )
    hit = tgt_all[:, None] == ids[None, :]
    row_max = jnp.max(logits, axis=1)
    local = jnp.stack(
        [
            row_max,
            jnp.sum(jnp.exp(logits - row_max[:, None]), axis=1),
            jnp.sum(jnp.where(hit, logits, 0.0), axis=1),
        ]
    )
    every = lax.all_to_all(jnp.broadcast_to(local[None], (devices,) + local.shape), ("dp", "vocab"), 0, 0, tiled=True)
    peak = jnp.max(every[:, 0], axis=0)
    denom = jnp.sum(every[:, 1] * jnp.exp(every[:, 0] - peak[None, :]), axis=0)
    target_logit = jnp.sum(every[:, 2], axis=0)
    lse = peak + jnp.log(denom)
    row_loss = lse - target_logit
    diff = jnp.exp(logits - lse[:, None]) - hit.astype(jnp.float32)
    grad = (diff / total_rows).astype(jnp.bfloat16)
    emb_grad = jnp.einsum("rv,rd->vd", grad, head_all, preferred_element_type=jnp.float32).astype(
        jnp.bfloat16
    )
    bias_grad = jnp.sum(diff, axis=0) / total_rows
    return (emb_grad, bias_grad, row_loss)


def solution(mesh):
    return jax.shard_map(
        body,
        mesh=mesh,
        in_specs=(
            P(("dp", "vocab"), None),
            P(("dp", "vocab"), None),
            P(("dp", "vocab")),
            P(("dp", "vocab"), None),
            P("dp", "vocab"),
            P("vocab"),
            P("vocab"),
            P("vocab"),
            P(("dp", "vocab"), None),
            P(("dp", "vocab")),
        ),
        out_specs=(P(("dp", "vocab"), None), P(("dp", "vocab")), P()),
        check_vma=False,
    )
```

```python
import jax
import jax.numpy as jnp
from jax import lax
from jax.sharding import PartitionSpec as P

MEAN = 2


EPS = 1e-05


def _pow2(n):
    return n & (n - 1) == 0


def _canon(axis, step, mine, theirs):
    upper = (lax.axis_index(axis) & step) != 0
    return jnp.where(upper, theirs, mine), jnp.where(upper, mine, theirs)


def _allreduce(x, axis, n, merge):
    step = 1
    while step < n:
        theirs = lax.ppermute(x, axis, [(a, a ^ step) for a in range(n)])
        lo, hi = _canon(axis, step, x, theirs)
        x = merge(lo, hi)
        step *= 2
    return x


def _allgather(x, axis, n, order=None):
    order = order or _steps(n)
    buf = x[None]
    for step in order:
        theirs = lax.ppermute(buf, axis, [(a, a ^ step) for a in range(n)])
        upper = (lax.axis_index(axis) & step) != 0
        buf = jnp.where(upper, jnp.concatenate([theirs, buf]), jnp.concatenate([buf, theirs]))
    block_of = [sum(((p >> t) & 1) * step for t, step in enumerate(order)) for p in range(n)]
    if block_of != list(range(n)):
        place = [block_of.index(k) for k in range(n)]
        buf = buf[jnp.array(place, dtype=jnp.int32)]
    return buf


def _steps(n):
    out, step = [], 1
    while step < n:
        out.append(step)
        step *= 2
    return out


def _reduce_scatter(x, axis, n, order=None):
    order = order or _steps(n)[::-1]
    idx = lax.axis_index(axis)
    bits = _steps(n)[::-1]
    rest = x.shape[1:]
    x = x.reshape((2,) * len(bits) + rest)
    for step in order:
        at = bits.index(step)
        upper = (idx & step) != 0
        low, high = jnp.take(x, 0, axis=at), jnp.take(x, 1, axis=at)
        kept = jnp.where(upper, high, low)
        sent = jnp.where(upper, low, high)
        theirs = lax.ppermute(sent, axis, [(a, a ^ step) for a in range(n)])
        lo, hi = _canon(axis, step, kept, theirs)
        x = lo + hi
        bits.pop(at)
    return x


def _pieces(t):
    return jnp.concatenate([t >> 16, (t >> 8) & 255, t & 255])


def _unpieces(p):
    return p[..., 0, :] * 65536 + p[..., 1, :] * 256 + p[..., 2, :]


def _add(lo, hi):
    return lo + hi


def _psum(x, axis, n):
    if _pow2(n):
        return _allreduce(x, axis, n, _add)
    return lax.psum(x, axis)


def _gather(x, axis, n, order=None):
    if _pow2(n):
        return _allgather(x, axis, n, order)
    return lax.all_gather(x, axis, axis=0, tiled=False)


def _softmax_merge(lo, hi):
    peak = jnp.maximum(lo[0], hi[0])
    total = lo[1] * jnp.exp(lo[0] - peak) + hi[1] * jnp.exp(hi[0] - peak)
    return jnp.stack([peak, total, lo[2] + hi[2]])


def body(
    hidden,
    positions,
    counts,
    targets,
    dense_weight,
    dense_bias,
    norm_gain,
    norm_shift,
    embedding,
    decoder_bias,
):
    ways = lax.axis_size("vocab")
    groups = lax.axis_size("dp")
    model = hidden.shape[1]
    slots = positions.shape[1]
    group_rows = MEAN * ways
    total_rows = groups * group_rows
    in_block = dense_weight.shape[0]
    tokens = hidden.shape[0]
    onehot = (positions[0][:, None] == jnp.arange(tokens, dtype=jnp.int32)[None, :]).astype(hidden.dtype)
    picked = jnp.dot(onehot, hidden, preferred_element_type=jnp.float32).astype(hidden.dtype)
    meta = jnp.zeros((in_block,), jnp.int32).at[0].set(counts[0])
    meta = lax.dynamic_update_slice(meta, _pieces(targets[0]), (1,))
    blocks = jnp.concatenate(
        [
            picked.reshape(slots, groups, in_block).transpose(1, 0, 2),
            jnp.broadcast_to(meta.astype(hidden.dtype), (groups, 1, in_block)),
        ],
        axis=1,
    )
    got = lax.all_to_all(blocks, "dp", 0, 0, tiled=True)
    got = _gather(got, "vocab", ways, _steps(ways)[::-1]).transpose(1, 0, 2, 3)
    slot_rows = got[:, :, :slots].reshape(groups, ways * slots, in_block)
    got_meta = got[:, :, slots, : 1 + 3 * slots].astype(jnp.int32)
    got_tgt = _unpieces(got_meta[:, :, 1:].reshape(groups, ways, 3, slots)).reshape(groups, ways * slots)
    slot_ids = jnp.tile(jnp.arange(slots, dtype=jnp.int32), ways)
    row_ids = jnp.arange(group_rows, dtype=jnp.int32)

    def choose(group_counts):
        count_of = jnp.repeat(group_counts, slots)
        start_of = jnp.repeat(jnp.cumsum(group_counts) - group_counts, slots)
        valid = slot_ids < count_of
        dest = start_of + slot_ids
        return (dest[None, :] == row_ids[:, None]) & valid[None, :]

    choosers = jax.vmap(choose)(got_meta[:, :, 0])
    rows_in = jnp.einsum(
        "grs,gsd->grd", choosers.astype(hidden.dtype), slot_rows, preferred_element_type=jnp.float32
    ).astype(hidden.dtype).reshape(total_rows, in_block)
    tgt_all = jnp.sum(jnp.where(choosers, got_tgt[:, None, :], 0), axis=2).reshape(total_rows)
    part = jnp.dot(rows_in, dense_weight, preferred_element_type=jnp.float32)
    act = jnp.sum(lax.all_to_all(part.reshape(groups, group_rows, -1), "dp", 0, 0, tiled=True), axis=0)
    act = jax.nn.gelu(act + dense_bias, approximate=False)
    pieces = _gather(jnp.concatenate([act, norm_gain[None], norm_shift[None]]), "vocab", ways, _steps(ways)[::-1])
    pieces = pieces.transpose(1, 0, 2).reshape(group_rows + 2, model)
    act, gain, shift = pieces[:group_rows], pieces[group_rows], pieces[group_rows + 1]
    mean = jnp.sum(act, axis=1) / model
    var = jnp.sum(act * act, axis=1) / model - mean * mean
    head_rows = ((act - mean[:, None]) * lax.rsqrt(var + EPS)[:, None] * gain + shift).astype(jnp.bfloat16)
    head_all = lax.all_to_all(
        jnp.broadcast_to(head_rows[None], (groups,) + head_rows.shape), "dp", 0, 0, tiled=True
    ).reshape(total_rows, model)
    devices = groups * ways
    vocab_rows = embedding.shape[0]
    first_id = (lax.axis_index("dp") * ways + lax.axis_index("vocab")) * vocab_rows
    ids = first_id + jnp.arange(vocab_rows, dtype=jnp.int32)
    logits = (
        jnp.einsum("rd,vd->rv", head_all, embedding, preferred_element_type=jnp.float32)
        + decoder_bias[None, :]
    )
    hit = tgt_all[:, None] == ids[None, :]
    row_max = jnp.max(logits, axis=1)
    local = jnp.stack(
        [
            row_max,
            jnp.sum(jnp.exp(logits - row_max[:, None]), axis=1),
            jnp.sum(jnp.where(hit, logits, 0.0), axis=1),
        ]
    )
    every = lax.all_to_all(jnp.broadcast_to(local[None], (devices,) + local.shape), ("dp", "vocab"), 0, 0, tiled=True)
    peak = jnp.max(every[:, 0], axis=0)
    denom = jnp.sum(every[:, 1] * jnp.exp(every[:, 0] - peak[None, :]), axis=0)
    target_logit = jnp.sum(every[:, 2], axis=0)
    lse = peak + jnp.log(denom)
    row_loss = lse - target_logit
    diff = jnp.exp(logits - lse[:, None]) - hit.astype(jnp.float32)
    grad = (diff / total_rows).astype(jnp.bfloat16)
    emb_grad = jnp.einsum("rv,rd->vd", grad, head_all, preferred_element_type=jnp.float32).astype(
        jnp.bfloat16
    )
    bias_grad = jnp.sum(diff, axis=0) / total_rows
    return (emb_grad, bias_grad, row_loss)


def solution(mesh):
    return jax.shard_map(
        body,
        mesh=mesh,
        in_specs=(
            P(("dp", "vocab"), None),
            P(("dp", "vocab"), None),
            P(("dp", "vocab")),
            P(("dp", "vocab"), None),
            P("dp", "vocab"),
            P("vocab"),
            P("vocab"),
            P("vocab"),
            P(("dp", "vocab"), None),
            P(("dp", "vocab")),
        ),
        out_specs=(P(("dp", "vocab"), None), P(("dp", "vocab")), P()),
        check_vma=False,
    )
```

```python
import jax
import jax.numpy as jnp
from jax import lax
from jax.sharding import PartitionSpec as P

MEAN = 2


EPS = 1e-05


def _pow2(n):
    return n & (n - 1) == 0


def _canon(axis, step, mine, theirs):
    upper = (lax.axis_index(axis) & step) != 0
    return jnp.where(upper, theirs, mine), jnp.where(upper, mine, theirs)


def _allreduce(x, axis, n, merge):
    step = 1
    while step < n:
        theirs = lax.ppermute(x, axis, [(a, a ^ step) for a in range(n)])
        lo, hi = _canon(axis, step, x, theirs)
        x = merge(lo, hi)
        step *= 2
    return x


def _allgather(x, axis, n, order=None):
    order = order or _steps(n)
    buf = x[None]
    for step in order:
        theirs = lax.ppermute(buf, axis, [(a, a ^ step) for a in range(n)])
        upper = (lax.axis_index(axis) & step) != 0
        buf = jnp.where(upper, jnp.concatenate([theirs, buf]), jnp.concatenate([buf, theirs]))
    block_of = [sum(((p >> t) & 1) * step for t, step in enumerate(order)) for p in range(n)]
    if block_of != list(range(n)):
        place = [block_of.index(k) for k in range(n)]
        buf = buf[jnp.array(place, dtype=jnp.int32)]
    return buf


def _steps(n):
    out, step = [], 1
    while step < n:
        out.append(step)
        step *= 2
    return out


def _reduce_scatter(x, axis, n, order=None):
    order = order or _steps(n)[::-1]
    idx = lax.axis_index(axis)
    bits = _steps(n)[::-1]
    rest = x.shape[1:]
    x = x.reshape((2,) * len(bits) + rest)
    for step in order:
        at = bits.index(step)
        upper = (idx & step) != 0
        low, high = jnp.take(x, 0, axis=at), jnp.take(x, 1, axis=at)
        kept = jnp.where(upper, high, low)
        sent = jnp.where(upper, low, high)
        theirs = lax.ppermute(sent, axis, [(a, a ^ step) for a in range(n)])
        lo, hi = _canon(axis, step, kept, theirs)
        x = lo + hi
        bits.pop(at)
    return x


def _pieces(t):
    return jnp.concatenate([t >> 16, (t >> 8) & 255, t & 255])


def _unpieces(p):
    return p[..., 0, :] * 65536 + p[..., 1, :] * 256 + p[..., 2, :]


def _add(lo, hi):
    return lo + hi


def _psum(x, axis, n):
    if _pow2(n):
        return _allreduce(x, axis, n, _add)
    return lax.psum(x, axis)


def _gather(x, axis, n, order=None):
    if _pow2(n):
        return _allgather(x, axis, n, order)
    return lax.all_gather(x, axis, axis=0, tiled=False)


def _softmax_merge(lo, hi):
    peak = jnp.maximum(lo[0], hi[0])
    total = lo[1] * jnp.exp(lo[0] - peak) + hi[1] * jnp.exp(hi[0] - peak)
    return jnp.stack([peak, total, lo[2] + hi[2]])


def body(
    hidden,
    positions,
    counts,
    targets,
    dense_weight,
    dense_bias,
    norm_gain,
    norm_shift,
    embedding,
    decoder_bias,
):
    ways = lax.axis_size("vocab")
    groups = lax.axis_size("dp")
    model = hidden.shape[1]
    slots = positions.shape[1]
    group_rows = MEAN * ways
    total_rows = groups * group_rows
    in_block = dense_weight.shape[0]
    tokens = hidden.shape[0]
    onehot = (positions[0][:, None] == jnp.arange(tokens, dtype=jnp.int32)[None, :]).astype(hidden.dtype)
    picked = jnp.dot(onehot, hidden, preferred_element_type=jnp.float32).astype(hidden.dtype)
    meta = jnp.zeros((in_block,), jnp.int32).at[0].set(counts[0])
    meta = lax.dynamic_update_slice(meta, _pieces(targets[0]), (1,))
    blocks = jnp.concatenate(
        [
            picked.reshape(slots, groups, in_block).transpose(1, 0, 2),
            jnp.broadcast_to(meta.astype(hidden.dtype), (groups, 1, in_block)),
        ],
        axis=1,
    )
    got = lax.all_to_all(jnp.repeat(blocks, ways, axis=0), ("dp", "vocab"), 0, 0, tiled=True)
    got = got.reshape(groups, ways, slots + 1, in_block)
    slot_rows = got[:, :, :slots].reshape(groups, ways * slots, in_block)
    got_meta = got[:, :, slots, : 1 + 3 * slots].astype(jnp.int32)
    got_tgt = _unpieces(got_meta[:, :, 1:].reshape(groups, ways, 3, slots)).reshape(groups, ways * slots)
    slot_ids = jnp.tile(jnp.arange(slots, dtype=jnp.int32), ways)
    row_ids = jnp.arange(group_rows, dtype=jnp.int32)

    def choose(group_counts):
        count_of = jnp.repeat(group_counts, slots)
        start_of = jnp.repeat(jnp.cumsum(group_counts) - group_counts, slots)
        valid = slot_ids < count_of
        dest = start_of + slot_ids
        return (dest[None, :] == row_ids[:, None]) & valid[None, :]

    choosers = jax.vmap(choose)(got_meta[:, :, 0])
    rows_in = jnp.einsum(
        "grs,gsd->grd", choosers.astype(hidden.dtype), slot_rows, preferred_element_type=jnp.float32
    ).astype(hidden.dtype).reshape(total_rows, in_block)
    tgt_all = jnp.sum(jnp.where(choosers, got_tgt[:, None, :], 0), axis=2).reshape(total_rows)
    part = jnp.dot(rows_in, dense_weight, preferred_element_type=jnp.float32)
    act = jnp.sum(lax.all_to_all(part.reshape(groups, group_rows, -1), "dp", 0, 0, tiled=True), axis=0)
    act = jax.nn.gelu(act + dense_bias, approximate=False)
    pieces = _gather(jnp.concatenate([act, norm_gain[None], norm_shift[None]]), "vocab", ways)
    pieces = pieces.transpose(1, 0, 2).reshape(group_rows + 2, model)
    act, gain, shift = pieces[:group_rows], pieces[group_rows], pieces[group_rows + 1]
    mean = jnp.sum(act, axis=1) / model
    var = jnp.sum(act * act, axis=1) / model - mean * mean
    head_rows = ((act - mean[:, None]) * lax.rsqrt(var + EPS)[:, None] * gain + shift).astype(jnp.bfloat16)
    head_all = lax.all_to_all(
        jnp.broadcast_to(head_rows[None], (groups,) + head_rows.shape), "dp", 0, 0, tiled=True
    ).reshape(total_rows, model)
    devices = groups * ways
    vocab_rows = embedding.shape[0]
    first_id = (lax.axis_index("dp") * ways + lax.axis_index("vocab")) * vocab_rows
    ids = first_id + jnp.arange(vocab_rows, dtype=jnp.int32)
    logits = (
        jnp.einsum("rd,vd->rv", head_all, embedding, preferred_element_type=jnp.float32)
        + decoder_bias[None, :]
    )
    hit = tgt_all[:, None] == ids[None, :]
    row_max = jnp.max(logits, axis=1)
    local = jnp.stack(
        [
            row_max,
            jnp.sum(jnp.exp(logits - row_max[:, None]), axis=1),
            jnp.sum(jnp.where(hit, logits, 0.0), axis=1),
        ]
    )
    every = lax.all_to_all(jnp.broadcast_to(local[None], (devices,) + local.shape), ("dp", "vocab"), 0, 0, tiled=True)
    peak = jnp.max(every[:, 0], axis=0)
    denom = jnp.sum(every[:, 1] * jnp.exp(every[:, 0] - peak[None, :]), axis=0)
    target_logit = jnp.sum(every[:, 2], axis=0)
    lse = peak + jnp.log(denom)
    row_loss = lse - target_logit
    diff = jnp.exp(logits - lse[:, None]) - hit.astype(jnp.float32)
    grad = (diff / total_rows).astype(jnp.bfloat16)
    emb_grad = jnp.einsum("rv,rd->vd", grad, head_all, preferred_element_type=jnp.float32).astype(
        jnp.bfloat16
    )
    bias_grad = jnp.sum(diff, axis=0) / total_rows
    return (emb_grad, bias_grad, row_loss)


def solution(mesh):
    return jax.shard_map(
        body,
        mesh=mesh,
        in_specs=(
            P(("dp", "vocab"), None),
            P(("dp", "vocab"), None),
            P(("dp", "vocab")),
            P(("dp", "vocab"), None),
            P("dp", "vocab"),
            P("vocab"),
            P("vocab"),
            P("vocab"),
            P(("dp", "vocab"), None),
            P(("dp", "vocab")),
        ),
        out_specs=(P(("dp", "vocab"), None), P(("dp", "vocab")), P()),
        check_vma=False,
    )
```

```python
import jax
import jax.numpy as jnp
from jax import lax
from jax.sharding import PartitionSpec as P

MEAN = 2


EPS = 1e-05


def _pow2(n):
    return n & (n - 1) == 0


def _canon(axis, step, mine, theirs):
    upper = (lax.axis_index(axis) & step) != 0
    return jnp.where(upper, theirs, mine), jnp.where(upper, mine, theirs)


def _allreduce(x, axis, n, merge):
    step = 1
    while step < n:
        theirs = lax.ppermute(x, axis, [(a, a ^ step) for a in range(n)])
        lo, hi = _canon(axis, step, x, theirs)
        x = merge(lo, hi)
        step *= 2
    return x


def _allgather(x, axis, n, order=None):
    order = order or _steps(n)
    buf = x[None]
    for step in order:
        theirs = lax.ppermute(buf, axis, [(a, a ^ step) for a in range(n)])
        upper = (lax.axis_index(axis) & step) != 0
        buf = jnp.where(upper, jnp.concatenate([theirs, buf]), jnp.concatenate([buf, theirs]))
    block_of = [sum(((p >> t) & 1) * step for t, step in enumerate(order)) for p in range(n)]
    if block_of != list(range(n)):
        place = [block_of.index(k) for k in range(n)]
        buf = buf[jnp.array(place, dtype=jnp.int32)]
    return buf


def _steps(n):
    out, step = [], 1
    while step < n:
        out.append(step)
        step *= 2
    return out


def _reduce_scatter(x, axis, n, order=None):
    order = order or _steps(n)[::-1]
    idx = lax.axis_index(axis)
    bits = _steps(n)[::-1]
    rest = x.shape[1:]
    x = x.reshape((2,) * len(bits) + rest)
    for step in order:
        at = bits.index(step)
        upper = (idx & step) != 0
        low, high = jnp.take(x, 0, axis=at), jnp.take(x, 1, axis=at)
        kept = jnp.where(upper, high, low)
        sent = jnp.where(upper, low, high)
        theirs = lax.ppermute(sent, axis, [(a, a ^ step) for a in range(n)])
        lo, hi = _canon(axis, step, kept, theirs)
        x = lo + hi
        bits.pop(at)
    return x


def _pieces(t):
    return jnp.concatenate([t >> 16, (t >> 8) & 255, t & 255])


def _unpieces(p):
    return p[..., 0, :] * 65536 + p[..., 1, :] * 256 + p[..., 2, :]


def _add(lo, hi):
    return lo + hi


def _psum(x, axis, n):
    if _pow2(n):
        return _allreduce(x, axis, n, _add)
    return lax.psum(x, axis)


def _gather(x, axis, n, order=None):
    if _pow2(n):
        return _allgather(x, axis, n, order)
    return lax.all_gather(x, axis, axis=0, tiled=False)


def _softmax_merge(lo, hi):
    peak = jnp.maximum(lo[0], hi[0])
    total = lo[1] * jnp.exp(lo[0] - peak) + hi[1] * jnp.exp(hi[0] - peak)
    return jnp.stack([peak, total, lo[2] + hi[2]])


def body(
    hidden,
    positions,
    counts,
    targets,
    dense_weight,
    dense_bias,
    norm_gain,
    norm_shift,
    embedding,
    decoder_bias,
):
    ways = lax.axis_size("vocab")
    groups = lax.axis_size("dp")
    model = hidden.shape[1]
    slots = positions.shape[1]
    group_rows = MEAN * ways
    total_rows = groups * group_rows
    in_block = dense_weight.shape[0]
    tokens = hidden.shape[0]
    onehot = (positions[0][:, None] == jnp.arange(tokens, dtype=jnp.int32)[None, :]).astype(hidden.dtype)
    picked = jnp.dot(onehot, hidden, preferred_element_type=jnp.float32).astype(hidden.dtype)
    meta = jnp.zeros((in_block,), jnp.int32).at[0].set(counts[0])
    meta = lax.dynamic_update_slice(meta, _pieces(targets[0]), (1,))
    blocks = jnp.concatenate(
        [
            picked.reshape(slots, groups, in_block).transpose(1, 0, 2),
            jnp.broadcast_to(meta.astype(hidden.dtype), (groups, 1, in_block)),
        ],
        axis=1,
    )
    got = lax.all_to_all(jnp.repeat(blocks, ways, axis=0), ("dp", "vocab"), 0, 0, tiled=True)
    got = got.reshape(groups, ways, slots + 1, in_block)
    slot_rows = got[:, :, :slots].reshape(groups, ways * slots, in_block)
    got_meta = got[:, :, slots, : 1 + 3 * slots].astype(jnp.int32)
    got_tgt = _unpieces(got_meta[:, :, 1:].reshape(groups, ways, 3, slots)).reshape(groups, ways * slots)
    slot_ids = jnp.tile(jnp.arange(slots, dtype=jnp.int32), ways)
    row_ids = jnp.arange(group_rows, dtype=jnp.int32)

    def choose(group_counts):
        count_of = jnp.repeat(group_counts, slots)
        start_of = jnp.repeat(jnp.cumsum(group_counts) - group_counts, slots)
        valid = slot_ids < count_of
        dest = start_of + slot_ids
        return (dest[None, :] == row_ids[:, None]) & valid[None, :]

    choosers = jax.vmap(choose)(got_meta[:, :, 0])
    rows_in = jnp.einsum(
        "grs,gsd->grd", choosers.astype(hidden.dtype), slot_rows, preferred_element_type=jnp.float32
    ).astype(hidden.dtype).reshape(total_rows, in_block)
    tgt_all = jnp.sum(jnp.where(choosers, got_tgt[:, None, :], 0), axis=2).reshape(total_rows)
    part = jnp.dot(rows_in, dense_weight, preferred_element_type=jnp.float32)
    act = jnp.sum(lax.all_to_all(part.reshape(groups, group_rows, -1), "dp", 0, 0, tiled=True), axis=0)
    act = jax.nn.gelu(act + dense_bias, approximate=False)
    devices = groups * ways
    every_act = lax.all_to_all(
        jnp.broadcast_to(act[None], (devices,) + act.shape), ("dp", "vocab"), 0, 0, tiled=True
    )
    act = every_act.reshape(groups, ways, group_rows, -1).transpose(0, 2, 1, 3).reshape(total_rows, model)
    affine = _gather(jnp.stack([norm_gain, norm_shift]), "vocab", ways).transpose(1, 0, 2).reshape(2, model)
    mean = jnp.sum(act, axis=1) / model
    var = jnp.sum(act * act, axis=1) / model - mean * mean
    head_all = ((act - mean[:, None]) * lax.rsqrt(var + EPS)[:, None] * affine[0] + affine[1]).astype(jnp.bfloat16)
    vocab_rows = embedding.shape[0]
    first_id = (lax.axis_index("dp") * ways + lax.axis_index("vocab")) * vocab_rows
    ids = first_id + jnp.arange(vocab_rows, dtype=jnp.int32)
    logits = (
        jnp.einsum("rd,vd->rv", head_all, embedding, preferred_element_type=jnp.float32)
        + decoder_bias[None, :]
    )
    hit = tgt_all[:, None] == ids[None, :]
    row_max = jnp.max(logits, axis=1)
    local = jnp.stack(
        [
            row_max,
            jnp.sum(jnp.exp(logits - row_max[:, None]), axis=1),
            jnp.sum(jnp.where(hit, logits, 0.0), axis=1),
        ]
    )
    every = lax.all_to_all(jnp.broadcast_to(local[None], (devices,) + local.shape), ("dp", "vocab"), 0, 0, tiled=True)
    peak = jnp.max(every[:, 0], axis=0)
    denom = jnp.sum(every[:, 1] * jnp.exp(every[:, 0] - peak[None, :]), axis=0)
    target_logit = jnp.sum(every[:, 2], axis=0)
    lse = peak + jnp.log(denom)
    row_loss = lse - target_logit
    diff = jnp.exp(logits - lse[:, None]) - hit.astype(jnp.float32)
    grad = (diff / total_rows).astype(jnp.bfloat16)
    emb_grad = jnp.einsum("rv,rd->vd", grad, head_all, preferred_element_type=jnp.float32).astype(
        jnp.bfloat16
    )
    bias_grad = jnp.sum(diff, axis=0) / total_rows
    return (emb_grad, bias_grad, row_loss)


def solution(mesh):
    return jax.shard_map(
        body,
        mesh=mesh,
        in_specs=(
            P(("dp", "vocab"), None),
            P(("dp", "vocab"), None),
            P(("dp", "vocab")),
            P(("dp", "vocab"), None),
            P("dp", "vocab"),
            P("vocab"),
            P("vocab"),
            P("vocab"),
            P(("dp", "vocab"), None),
            P(("dp", "vocab")),
        ),
        out_specs=(P(("dp", "vocab"), None), P(("dp", "vocab")), P()),
        check_vma=False,
    )
```

```python
import jax
import jax.numpy as jnp
from jax import lax
from jax.sharding import PartitionSpec as P

MEAN = 2


EPS = 1e-05


def _pow2(n):
    return n & (n - 1) == 0


def _canon(axis, step, mine, theirs):
    upper = (lax.axis_index(axis) & step) != 0
    return jnp.where(upper, theirs, mine), jnp.where(upper, mine, theirs)


def _allreduce(x, axis, n, merge):
    step = 1
    while step < n:
        theirs = lax.ppermute(x, axis, [(a, a ^ step) for a in range(n)])
        lo, hi = _canon(axis, step, x, theirs)
        x = merge(lo, hi)
        step *= 2
    return x


def _allgather(x, axis, n, order=None):
    order = order or _steps(n)
    buf = x[None]
    for step in order:
        theirs = lax.ppermute(buf, axis, [(a, a ^ step) for a in range(n)])
        upper = (lax.axis_index(axis) & step) != 0
        buf = jnp.where(upper, jnp.concatenate([theirs, buf]), jnp.concatenate([buf, theirs]))
    block_of = [sum(((p >> t) & 1) * step for t, step in enumerate(order)) for p in range(n)]
    if block_of != list(range(n)):
        place = [block_of.index(k) for k in range(n)]
        buf = buf[jnp.array(place, dtype=jnp.int32)]
    return buf


def _steps(n):
    out, step = [], 1
    while step < n:
        out.append(step)
        step *= 2
    return out


def _reduce_scatter(x, axis, n, order=None):
    order = order or _steps(n)[::-1]
    idx = lax.axis_index(axis)
    bits = _steps(n)[::-1]
    rest = x.shape[1:]
    x = x.reshape((2,) * len(bits) + rest)
    for step in order:
        at = bits.index(step)
        upper = (idx & step) != 0
        low, high = jnp.take(x, 0, axis=at), jnp.take(x, 1, axis=at)
        kept = jnp.where(upper, high, low)
        sent = jnp.where(upper, low, high)
        theirs = lax.ppermute(sent, axis, [(a, a ^ step) for a in range(n)])
        lo, hi = _canon(axis, step, kept, theirs)
        x = lo + hi
        bits.pop(at)
    return x


def _pieces(t):
    return jnp.concatenate([t >> 16, (t >> 8) & 255, t & 255])


def _unpieces(p):
    return p[..., 0, :] * 65536 + p[..., 1, :] * 256 + p[..., 2, :]


def _add(lo, hi):
    return lo + hi


def _psum(x, axis, n):
    if _pow2(n):
        return _allreduce(x, axis, n, _add)
    return lax.psum(x, axis)


def _gather(x, axis, n, order=None):
    if _pow2(n):
        return _allgather(x, axis, n, order)
    return lax.all_gather(x, axis, axis=0, tiled=False)


def _softmax_merge(lo, hi):
    peak = jnp.maximum(lo[0], hi[0])
    total = lo[1] * jnp.exp(lo[0] - peak) + hi[1] * jnp.exp(hi[0] - peak)
    return jnp.stack([peak, total, lo[2] + hi[2]])


def body(
    hidden,
    positions,
    counts,
    targets,
    dense_weight,
    dense_bias,
    norm_gain,
    norm_shift,
    embedding,
    decoder_bias,
):
    ways = lax.axis_size("vocab")
    groups = lax.axis_size("dp")
    model = hidden.shape[1]
    slots = positions.shape[1]
    group_rows = MEAN * ways
    total_rows = groups * group_rows
    in_block = dense_weight.shape[0]
    tokens = hidden.shape[0]
    onehot = (positions[0][:, None] == jnp.arange(tokens, dtype=jnp.int32)[None, :]).astype(hidden.dtype)
    picked = jnp.dot(onehot, hidden, preferred_element_type=jnp.float32).astype(hidden.dtype)
    meta = jnp.zeros((in_block,), jnp.int32).at[0].set(counts[0])
    meta = lax.dynamic_update_slice(meta, _pieces(targets[0]), (1,))
    blocks = jnp.concatenate(
        [
            picked.reshape(slots, groups, in_block).transpose(1, 0, 2),
            jnp.broadcast_to(meta.astype(hidden.dtype), (groups, 1, in_block)),
        ],
        axis=1,
    )
    got = lax.all_to_all(jnp.repeat(blocks, ways, axis=0), ("dp", "vocab"), 0, 0, tiled=True)
    got = got.reshape(groups, ways, slots + 1, in_block)
    slot_rows = got[:, :, :slots].reshape(groups, ways * slots, in_block)
    got_meta = got[:, :, slots, : 1 + 3 * slots].astype(jnp.int32)
    got_tgt = _unpieces(got_meta[:, :, 1:].reshape(groups, ways, 3, slots)).reshape(groups, ways * slots)
    slot_ids = jnp.tile(jnp.arange(slots, dtype=jnp.int32), ways)
    row_ids = jnp.arange(group_rows, dtype=jnp.int32)

    def choose(group_counts):
        count_of = jnp.repeat(group_counts, slots)
        start_of = jnp.repeat(jnp.cumsum(group_counts) - group_counts, slots)
        valid = slot_ids < count_of
        dest = start_of + slot_ids
        return (dest[None, :] == row_ids[:, None]) & valid[None, :]

    choosers = jax.vmap(choose)(got_meta[:, :, 0])
    rows_in = jnp.einsum(
        "grs,gsd->grd", choosers.astype(hidden.dtype), slot_rows, preferred_element_type=jnp.float32
    ).astype(hidden.dtype).reshape(total_rows, in_block)
    tgt_all = jnp.sum(jnp.where(choosers, got_tgt[:, None, :], 0), axis=2).reshape(total_rows)
    part = jnp.dot(rows_in, dense_weight, preferred_element_type=jnp.float32)
    act = jnp.sum(lax.all_to_all(part.reshape(groups, group_rows, -1), "dp", 0, 0, tiled=True), axis=0)
    act = jax.nn.gelu(act + dense_bias, approximate=False)
    pieces = _gather(jnp.concatenate([act, norm_gain[None], norm_shift[None]]), "vocab", ways)
    pieces = pieces.transpose(1, 0, 2).reshape(group_rows + 2, model)
    act, gain, shift = pieces[:group_rows], pieces[group_rows], pieces[group_rows + 1]
    mean = jnp.sum(act, axis=1) / model
    var = jnp.sum(act * act, axis=1) / model - mean * mean
    head_rows = ((act - mean[:, None]) * lax.rsqrt(var + EPS)[:, None] * gain + shift).astype(jnp.bfloat16)
    feat = model // ways
    head_blk = lax.dynamic_slice_in_dim(head_rows, lax.axis_index("vocab") * feat, feat, axis=1)
    head_cols = lax.all_to_all(
        jnp.broadcast_to(head_blk[None], (groups,) + head_blk.shape), "dp", 0, 0, tiled=True
    ).reshape(total_rows, feat)
    head_all = _gather(head_cols, "vocab", ways, _steps(ways)[::-1]).transpose(1, 0, 2).reshape(total_rows, model)
    devices = groups * ways
    vocab_rows = embedding.shape[0]
    first_id = (lax.axis_index("dp") * ways + lax.axis_index("vocab")) * vocab_rows
    ids = first_id + jnp.arange(vocab_rows, dtype=jnp.int32)
    logits = (
        jnp.einsum("rd,vd->rv", head_all, embedding, preferred_element_type=jnp.float32)
        + decoder_bias[None, :]
    )
    hit = tgt_all[:, None] == ids[None, :]
    row_max = jnp.max(logits, axis=1)
    local = jnp.stack(
        [
            row_max,
            jnp.sum(jnp.exp(logits - row_max[:, None]), axis=1),
            jnp.sum(jnp.where(hit, logits, 0.0), axis=1),
        ]
    )
    every = lax.all_to_all(jnp.broadcast_to(local[None], (devices,) + local.shape), ("dp", "vocab"), 0, 0, tiled=True)
    peak = jnp.max(every[:, 0], axis=0)
    denom = jnp.sum(every[:, 1] * jnp.exp(every[:, 0] - peak[None, :]), axis=0)
    target_logit = jnp.sum(every[:, 2], axis=0)
    lse = peak + jnp.log(denom)
    row_loss = lse - target_logit
    diff = jnp.exp(logits - lse[:, None]) - hit.astype(jnp.float32)
    grad = (diff / total_rows).astype(jnp.bfloat16)
    emb_grad = jnp.einsum("rv,rd->vd", grad, head_all, preferred_element_type=jnp.float32).astype(
        jnp.bfloat16
    )
    bias_grad = jnp.sum(diff, axis=0) / total_rows
    return (emb_grad, bias_grad, row_loss)


def solution(mesh):
    return jax.shard_map(
        body,
        mesh=mesh,
        in_specs=(
            P(("dp", "vocab"), None),
            P(("dp", "vocab"), None),
            P(("dp", "vocab")),
            P(("dp", "vocab"), None),
            P("dp", "vocab"),
            P("vocab"),
            P("vocab"),
            P("vocab"),
            P(("dp", "vocab"), None),
            P(("dp", "vocab")),
        ),
        out_specs=(P(("dp", "vocab"), None), P(("dp", "vocab")), P()),
        check_vma=False,
    )
```

```python
import jax
import jax.numpy as jnp
from jax import lax
from jax.sharding import PartitionSpec as P

MEAN = 2


EPS = 1e-05


def _pow2(n):
    return n & (n - 1) == 0


def _canon(axis, step, mine, theirs):
    upper = (lax.axis_index(axis) & step) != 0
    return jnp.where(upper, theirs, mine), jnp.where(upper, mine, theirs)


def _allreduce(x, axis, n, merge):
    step = 1
    while step < n:
        theirs = lax.ppermute(x, axis, [(a, a ^ step) for a in range(n)])
        lo, hi = _canon(axis, step, x, theirs)
        x = merge(lo, hi)
        step *= 2
    return x


def _allgather(x, axis, n, order=None):
    order = order or _steps(n)
    buf = x[None]
    for step in order:
        theirs = lax.ppermute(buf, axis, [(a, a ^ step) for a in range(n)])
        upper = (lax.axis_index(axis) & step) != 0
        buf = jnp.where(upper, jnp.concatenate([theirs, buf]), jnp.concatenate([buf, theirs]))
    block_of = [sum(((p >> t) & 1) * step for t, step in enumerate(order)) for p in range(n)]
    if block_of != list(range(n)):
        place = [block_of.index(k) for k in range(n)]
        buf = buf[jnp.array(place, dtype=jnp.int32)]
    return buf


def _steps(n):
    out, step = [], 1
    while step < n:
        out.append(step)
        step *= 2
    return out


def _reduce_scatter(x, axis, n, order=None):
    order = order or _steps(n)[::-1]
    idx = lax.axis_index(axis)
    bits = _steps(n)[::-1]
    rest = x.shape[1:]
    x = x.reshape((2,) * len(bits) + rest)
    for step in order:
        at = bits.index(step)
        upper = (idx & step) != 0
        low, high = jnp.take(x, 0, axis=at), jnp.take(x, 1, axis=at)
        kept = jnp.where(upper, high, low)
        sent = jnp.where(upper, low, high)
        theirs = lax.ppermute(sent, axis, [(a, a ^ step) for a in range(n)])
        lo, hi = _canon(axis, step, kept, theirs)
        x = lo + hi
        bits.pop(at)
    return x


def _pieces(t):
    return jnp.concatenate([t >> 16, (t >> 8) & 255, t & 255])


def _unpieces(p):
    return p[..., 0, :] * 65536 + p[..., 1, :] * 256 + p[..., 2, :]


def _add(lo, hi):
    return lo + hi


def _psum(x, axis, n):
    if _pow2(n):
        return _allreduce(x, axis, n, _add)
    return lax.psum(x, axis)


def _gather(x, axis, n, order=None):
    if _pow2(n):
        return _allgather(x, axis, n, order)
    return lax.all_gather(x, axis, axis=0, tiled=False)


def _softmax_merge(lo, hi):
    peak = jnp.maximum(lo[0], hi[0])
    total = lo[1] * jnp.exp(lo[0] - peak) + hi[1] * jnp.exp(hi[0] - peak)
    return jnp.stack([peak, total, lo[2] + hi[2]])


def body(
    hidden,
    positions,
    counts,
    targets,
    dense_weight,
    dense_bias,
    norm_gain,
    norm_shift,
    embedding,
    decoder_bias,
):
    ways = lax.axis_size("vocab")
    groups = lax.axis_size("dp")
    model = hidden.shape[1]
    slots = positions.shape[1]
    group_rows = MEAN * ways
    total_rows = groups * group_rows
    in_block = dense_weight.shape[0]
    tokens = hidden.shape[0]
    onehot = (positions[0][:, None] == jnp.arange(tokens, dtype=jnp.int32)[None, :]).astype(hidden.dtype)
    picked = jnp.einsum(
        "sk,kbd->bsd", onehot, hidden.reshape(tokens, -1, dense_weight.shape[0]), preferred_element_type=jnp.float32
    ).astype(hidden.dtype)
    meta = jnp.zeros((in_block,), jnp.int32).at[0].set(counts[0])
    meta = lax.dynamic_update_slice(meta, _pieces(targets[0]), (1,))
    blocks = jnp.concatenate(
        [
            picked,
            jnp.broadcast_to(meta.astype(hidden.dtype), (groups, 1, in_block)),
        ],
        axis=1,
    )
    got = lax.all_to_all(jnp.repeat(blocks, ways, axis=0), ("dp", "vocab"), 0, 0, tiled=True)
    got = got.reshape(groups, ways, slots + 1, in_block)
    slot_rows = got[:, :, :slots].reshape(groups, ways * slots, in_block)
    got_meta = got[:, :, slots, : 1 + 3 * slots].astype(jnp.int32)
    got_tgt = _unpieces(got_meta[:, :, 1:].reshape(groups, ways, 3, slots)).reshape(groups, ways * slots)
    slot_ids = jnp.tile(jnp.arange(slots, dtype=jnp.int32), ways)
    row_ids = jnp.arange(group_rows, dtype=jnp.int32)

    def choose(group_counts):
        count_of = jnp.repeat(group_counts, slots)
        start_of = jnp.repeat(jnp.cumsum(group_counts) - group_counts, slots)
        valid = slot_ids < count_of
        dest = start_of + slot_ids
        return (dest[None, :] == row_ids[:, None]) & valid[None, :]

    choosers = jax.vmap(choose)(got_meta[:, :, 0])
    rows_in = jnp.einsum(
        "grs,gsd->grd", choosers.astype(hidden.dtype), slot_rows, preferred_element_type=jnp.float32
    ).astype(hidden.dtype).reshape(total_rows, in_block)
    tgt_all = jnp.sum(jnp.where(choosers, got_tgt[:, None, :], 0), axis=2).reshape(total_rows)
    part = jnp.dot(rows_in, dense_weight, preferred_element_type=jnp.float32)
    act = jnp.sum(lax.all_to_all(part.reshape(groups, group_rows, -1), "dp", 0, 0, tiled=True), axis=0)
    act = jax.nn.gelu(act + dense_bias, approximate=False)
    pieces = _gather(jnp.concatenate([act, norm_gain[None], norm_shift[None]]), "vocab", ways)
    pieces = pieces.transpose(1, 0, 2).reshape(group_rows + 2, model)
    act, gain, shift = pieces[:group_rows], pieces[group_rows], pieces[group_rows + 1]
    mean = jnp.sum(act, axis=1) / model
    var = jnp.sum(act * act, axis=1) / model - mean * mean
    head_rows = ((act - mean[:, None]) * lax.rsqrt(var + EPS)[:, None] * gain + shift).astype(jnp.bfloat16)
    feat = model // ways
    head_blk = lax.dynamic_slice_in_dim(head_rows, lax.axis_index("vocab") * feat, feat, axis=1)
    head_cols = lax.all_to_all(
        jnp.broadcast_to(head_blk[None], (groups,) + head_blk.shape), "dp", 0, 0, tiled=True
    ).reshape(total_rows, feat)
    head_all = _gather(head_cols, "vocab", ways, _steps(ways)[::-1]).transpose(1, 0, 2).reshape(total_rows, model)
    devices = groups * ways
    vocab_rows = embedding.shape[0]
    first_id = (lax.axis_index("dp") * ways + lax.axis_index("vocab")) * vocab_rows
    ids = first_id + jnp.arange(vocab_rows, dtype=jnp.int32)
    logits = (
        jnp.einsum("rd,vd->rv", head_all, embedding, preferred_element_type=jnp.float32)
        + decoder_bias[None, :]
    )
    hit = tgt_all[:, None] == ids[None, :]
    row_max = jnp.max(logits, axis=1)
    local = jnp.stack(
        [
            row_max,
            jnp.sum(jnp.exp(logits - row_max[:, None]), axis=1),
            jnp.sum(jnp.where(hit, logits, 0.0), axis=1),
        ]
    )
    every = lax.all_to_all(jnp.broadcast_to(local[None], (devices,) + local.shape), ("dp", "vocab"), 0, 0, tiled=True)
    peak = jnp.max(every[:, 0], axis=0)
    denom = jnp.sum(every[:, 1] * jnp.exp(every[:, 0] - peak[None, :]), axis=0)
    target_logit = jnp.sum(every[:, 2], axis=0)
    lse = peak + jnp.log(denom)
    row_loss = lse - target_logit
    diff = jnp.exp(logits - lse[:, None]) - hit.astype(jnp.float32)
    grad = (diff / total_rows).astype(jnp.bfloat16)
    emb_grad = jnp.einsum("rv,rd->vd", grad, head_all, preferred_element_type=jnp.float32).astype(
        jnp.bfloat16
    )
    bias_grad = jnp.sum(diff, axis=0) / total_rows
    return (emb_grad, bias_grad, row_loss)


def solution(mesh):
    return jax.shard_map(
        body,
        mesh=mesh,
        in_specs=(
            P(("dp", "vocab"), None),
            P(("dp", "vocab"), None),
            P(("dp", "vocab")),
            P(("dp", "vocab"), None),
            P("dp", "vocab"),
            P("vocab"),
            P("vocab"),
            P("vocab"),
            P(("dp", "vocab"), None),
            P(("dp", "vocab")),
        ),
        out_specs=(P(("dp", "vocab"), None), P(("dp", "vocab")), P()),
        check_vma=False,
    )
```
